256 devices in a mesh: cam: 8 (over z_lo, x), pt: 32 (over y, z_hi, core).
Axes of the slice: x: 4, y: 4, z: 8 (z_hi: 4, z_lo: 2; z = z_hi * 2 + z_lo), core: 2. Of those that a mesh axis runs over, the one named last changes fastest.
Arguments:
- cameras: float32 [9, 32768], P(None, ('cam', 'pt')), as said below
- cam_first: float32 [9, 32768], P(None, ('cam', 'pt')), may hold values from -0.03 to 0.03
- cam_second: float32 [9, 32768], P(None, ('cam', 'pt')), may hold values from 0.001 to 0.1
- points: float32 [3, 1048576], P(None, ('pt', 'cam')), may hold values from -1 to 1
- pt_first: float32 [3, 1048576], P(None, ('pt', 'cam')), may hold values from -0.03 to 0.03
- pt_second: float32 [3, 1048576], P(None, ('pt', 'cam')), may hold values from 0.001 to 0.1
- observed: float32 [2, 3145728], P(None, ('cam', 'pt')), may hold values from -3 to 3
- tile_camera: int32 [12288], P(('cam', 'pt')), may hold values from 0 to 4095
- point_index: int32 [3145728], P(('cam', 'pt')), may hold values from 0 to 32767
- tile_count: int32 [12288], P(('cam', 'pt')), may hold values from 1 to 256, as said below
Outputs:
- new_cameras: float32 [9, 32768], P(None, ('cam', 'pt'))
- new_cam_first: float32 [9, 32768], P(None, ('cam', 'pt'))
- new_cam_second: float32 [9, 32768], P(None, ('cam', 'pt'))
- new_points: float32 [3, 1048576], P(None, ('pt', 'cam'))
- new_pt_first: float32 [3, 1048576], P(None, ('pt', 'cam'))
- new_pt_second: float32 [3, 1048576], P(None, ('pt', 'cam'))
- final_residual: float32 [2, 3145728], P(None, ('cam', 'pt'))
- final_weight: float32 [3145728], P(('cam', 'pt'))
The draws below stay inside these ranges and needn't reach their ends.
Inputs may be any that keep to these rules, and one draw needn't show every extreme that they name: `cameras`: rotation vectors within 0.2 a component, translations within 1 sideways and 4 to 6 in depth, focal lengths 0.8 to 1.2, distortion coefficients within 0.05. `tile_count`: some tile holds exactly 256 live slots; the loads differ from device to device.
All inputs are finite; a program needn't handle non-finite values.
Results may differ from the reference program's by a relative error of at most 0.00002.
Values sent between devices are 32-bit elements; how exact they have to be, the bound alone decides.
No kernel may reach another device: no remote copies, remote signals or barrier semaphores. Data moves between devices by JAX's collectives and lax.ppermute only.
A program may use at most 64 MiB of HBM per device.

```python
import math
import jax
import jax.numpy as jnp
from jax import lax

TILES_DEV = 48
TILE = 256
STEP = 10
CAM_BLK = 4096
PT_BLK = 32768
CAMS = 32768
PTS = 1048576
TILES = 12288
OBS = 3145728
N_PT = 32


def draw_cameras(key, part):
    keys = jax.random.split(jax.random.fold_in(key, 11), 5)
    rotation = jax.random.uniform(keys[0], (3, CAMS), jnp.float32, -0.2, 0.2)
    sideways = jax.random.uniform(keys[1], (2, CAMS), jnp.float32, -1.0, 1.0)
    depth = jax.random.uniform(keys[2], (1, CAMS), jnp.float32, 4.0, 6.0)
    focal = jax.random.uniform(keys[3], (1, CAMS), jnp.float32, 0.8, 1.2)
    distortion = jax.random.uniform(keys[4], (2, CAMS), jnp.float32, -0.05, 0.05)
    return jnp.concatenate([rotation, sideways, depth, focal, distortion], axis=0)


def draw_tile_count(key, part):
    keys = jax.random.split(jax.random.fold_in(key, 23), 3)
    device_count = TILES // TILES_DEV
    limits = jax.random.randint(keys[0], (device_count, 1), TILE // 4, TILE + 1)
    raw = jax.random.randint(keys[1], (device_count, TILES_DEV), 0, 1048576)
    counts = (1 + raw % limits).reshape(-1)
    chosen = jax.random.randint(keys[2], (), 0, TILES)
    places = jnp.arange(TILES, dtype=jnp.int32)
    return jnp.where(places == chosen, TILE, counts).astype(jnp.int32)


def touch_ends(result, own_key, smallest, largest):
    spot = [jax.random.randint(jax.random.fold_in(own_key, axis), (), 0, length) for axis, length in enumerate(result.shape)]
    longest = result.shape.index(max(result.shape))
    neighbour = spot[:longest] + [(spot[longest] + 1) % result.shape[longest]] + spot[longest + 1:]
    return result.at[tuple(spot)].set(smallest).at[tuple(neighbour)].set(largest)


def levels(stream_key, dims, pieces, smallest, high):
    def one(position, shards_of):
        draws = jax.random.uniform(jax.random.fold_in(jax.random.fold_in(stream_key, 6), position), (shards_of,), jnp.float32, smallest / len(pieces), high / len(pieces))
        return jnp.repeat(jnp.exp(draws), dims[position] // shards_of).reshape((-1,) + (1,) * (len(dims) - position - 1))

    loudness = one(*pieces[0])
    for cut in pieces[1:]:
        loudness = loudness * one(*cut)
    return loudness


def bell_draw(own_key, dims, scale, reach, shards=(), kind=jnp.bfloat16):
    factor_of = levels(own_key, dims, shards, -0.22, 0.18) if shards else 1.0
    values = jax.random.normal(own_key, dims, jnp.float32) * scale * factor_of
    return jnp.minimum(jnp.maximum(values, -reach), reach).astype(kind)


def setup_inputs(seed: int = 0) -> dict:
    key_list = jax.random.split(jax.random.key(seed), 11)
    return {
        "cameras": draw_cameras(jax.random.fold_in(key_list[10], 71), 0),
        "cam_first": jnp.clip(jax.random.uniform(key_list[1], (9, CAMS), jnp.float32, -0.03, 0.03) * levels(key_list[1], (9, CAMS), ((1, 256),), -0.4, 0.0), -0.03, 0.03),
        "cam_second": jnp.clip(jnp.exp(math.log(0.1) - 4.6051702 * jax.random.uniform(key_list[2], (9, CAMS), jnp.float32) ** levels(key_list[2], (9, CAMS), ((1, 256),), -0.2, 0.2)), 0.001, 0.1),
        "points": jnp.clip(jax.random.uniform(key_list[3], (3, PTS), jnp.float32, -1.0, 1.0) * levels(key_list[3], (3, PTS), ((1, 256),), -0.4, 0.0), -1.0, 1.0),
        "pt_first": jnp.clip(jax.random.uniform(key_list[4], (3, PTS), jnp.float32, -0.03, 0.03) * levels(key_list[4], (3, PTS), ((1, 256),), -0.4, 0.0), -0.03, 0.03),
        "pt_second": jnp.clip(jnp.exp(math.log(0.1) - 4.6051702 * jax.random.uniform(key_list[5], (3, PTS), jnp.float32) ** levels(key_list[5], (3, PTS), ((1, 256),), -0.2, 0.2)), 0.001, 0.1),
        "observed": bell_draw(key_list[6], (2, OBS), 0.5, 3.0, ((1, 256),), jnp.float32),
        "tile_camera": touch_ends(jax.random.randint(key_list[7], (TILES,), 0, CAM_BLK), jax.random.fold_in(key_list[7], 1), 0, CAM_BLK - 1).astype(jnp.int32),
        "point_index": touch_ends(jax.random.randint(key_list[8], (OBS,), 0, PT_BLK), jax.random.fold_in(key_list[8], 1), 0, PT_BLK - 1).astype(jnp.int32),
        "tile_count": draw_tile_count(jax.random.fold_in(key_list[10], 71), 0),
    }


def project(camera_tile, point_obs, observed):
    axis_angle = camera_tile[0:3]
    theta_sq = lax.optimization_barrier(jnp.sum(axis_angle * axis_angle, axis=0))
    sine_term = 1.0 - theta_sq / 6.0 + theta_sq * theta_sq / 120.0 - theta_sq * theta_sq * theta_sq / 5040.0 + theta_sq * theta_sq * theta_sq * theta_sq / 362880.0
    cosine_term = 0.5 - theta_sq / 24.0 + theta_sq * theta_sq / 720.0 - theta_sq * theta_sq * theta_sq / 40320.0 + theta_sq * theta_sq * theta_sq * theta_sq / 3628800.0
    crossed = jnp.stack([axis_angle[1] * point_obs[2] - axis_angle[2] * point_obs[1], axis_angle[2] * point_obs[0] - axis_angle[0] * point_obs[2], axis_angle[0] * point_obs[1] - axis_angle[1] * point_obs[0]])
    inner = lax.optimization_barrier(jnp.sum(axis_angle * point_obs, axis=0))
    camera_frame = point_obs + sine_term * crossed + cosine_term * (axis_angle * inner - theta_sq * point_obs) + camera_tile[3:6]
    horizontal = camera_frame[0] / camera_frame[2]
    vertical = camera_frame[1] / camera_frame[2]
    radius_sq = horizontal * horizontal + vertical * vertical
    scale_term = camera_tile[6] * (1.0 + camera_tile[7] * radius_sq + camera_tile[8] * radius_sq * radius_sq)
    return jnp.stack([scale_term * horizontal - observed[0], scale_term * vertical - observed[1]])

def reweight(residual):
    return 1.0 / (1.0 + residual[0] * residual[0] + residual[1] * residual[1])

def adam_step(current, moment_one, moment_two, gradient):
    moment_one = 0.9 * moment_one + 0.1 * gradient
    moment_two = 0.999 * moment_two + 0.001 * gradient * gradient
    corrected_one = moment_one / (1.0 - 0.9 ** STEP)
    corrected_two = moment_two / (1.0 - 0.999 ** STEP)
    return (current - 0.05 * corrected_one / (jnp.sqrt(corrected_two) + 1e-08), moment_one, moment_two)

def reference(cameras, cam_first, cam_second, points, pt_first, pt_second, observed, tile_camera, point_index, tile_count):
    tile_all = tile_count.shape[0]
    tile_len = observed.shape[1] // tile_all
    device = jnp.arange(tile_all, dtype=jnp.int32) // TILES_DEV
    camera_global = (device // N_PT * CAM_BLK + tile_camera).astype(jnp.int32)
    point_base = (device % N_PT * PT_BLK).astype(jnp.int32)
    point_global = (point_base[:, None] + point_index.reshape(tile_all, tile_len)).astype(jnp.int32).reshape(-1)
    obs_grid = observed.reshape(2, tile_all, tile_len)
    slot = lax.broadcasted_iota(jnp.int32, (tile_all, tile_len), 1)
    valid_mask = (slot < tile_count[:, None]).astype(cameras.dtype)

    def residuals(camera_all, point_all):
        camera_tile = jnp.take(camera_all, camera_global, axis=1)[:, :, None]
        point_obs = jnp.take(point_all, point_global, axis=1).reshape(3, tile_all, tile_len)
        return project(camera_tile, point_obs, obs_grid)
    residual, pullback = jax.vjp(residuals, cameras, points)
    cotangent = residual * (reweight(residual) * valid_mask)
    camera_grad, point_grad = pullback(cotangent)
    new_cameras, new_cam_first, new_cam_second = adam_step(cameras, cam_first, cam_second, camera_grad)
    new_points, new_pt_first, new_pt_second = adam_step(points, pt_first, pt_second, point_grad)
    final = residuals(new_cameras, new_points)
    final_weight = (reweight(final) * valid_mask).reshape(-1)
    final_residual = (final * valid_mask).reshape(2, -1)
    return (new_cameras, new_cam_first, new_cam_second, new_points, new_pt_first, new_pt_second, final_residual, final_weight)
```

```python
import jax
import jax.numpy as jnp
from jax import lax
from jax.sharding import PartitionSpec as P

STEP = 10


def project(camera_tile, point_obs, observed):
    axis_angle = camera_tile[0:3]
    theta_sq = jnp.sum(axis_angle * axis_angle, axis=0)
    sine_term = (
        1.0
        - theta_sq / 6.0
        + theta_sq * theta_sq / 120.0
        - theta_sq * theta_sq * theta_sq / 5040.0
        + theta_sq * theta_sq * theta_sq * theta_sq / 362880.0
    )
    cosine_term = (
        0.5
        - theta_sq / 24.0
        + theta_sq * theta_sq / 720.0
        - theta_sq * theta_sq * theta_sq / 40320.0
        + theta_sq * theta_sq * theta_sq * theta_sq / 3628800.0
    )
    crossed = jnp.stack(
        [
            axis_angle[1] * point_obs[2] - axis_angle[2] * point_obs[1],
            axis_angle[2] * point_obs[0] - axis_angle[0] * point_obs[2],
            axis_angle[0] * point_obs[1] - axis_angle[1] * point_obs[0],
        ]
    )
    inner = jnp.sum(axis_angle * point_obs, axis=0)
    camera_frame = (
        point_obs
        + sine_term * crossed
        + cosine_term * (axis_angle * inner - theta_sq * point_obs)
        + camera_tile[3:6]
    )
    horizontal = camera_frame[0] / camera_frame[2]
    vertical = camera_frame[1] / camera_frame[2]
    radius_sq = horizontal * horizontal + vertical * vertical
    scale_term = camera_tile[6] * (
        1.0 + camera_tile[7] * radius_sq + camera_tile[8] * radius_sq * radius_sq
    )
    return jnp.stack([scale_term * horizontal - observed[0], scale_term * vertical - observed[1]])


def reweight(residual):
    return 1.0 / (1.0 + residual[0] * residual[0] + residual[1] * residual[1])


def adam_step(current, moment_one, moment_two, gradient):
    moment_one = 0.9 * moment_one + 0.1 * gradient
    moment_two = 0.999 * moment_two + 0.001 * gradient * gradient
    corrected_one = moment_one / (1.0 - 0.9**STEP)
    corrected_two = moment_two / (1.0 - 0.999**STEP)
    return (
        current - 0.05 * corrected_one / (jnp.sqrt(corrected_two) + 1e-08),
        moment_one,
        moment_two,
    )


def on_device(
    cameras,
    cam_first,
    cam_second,
    points,
    pt_first,
    pt_second,
    observed,
    tile_camera,
    point_index,
    tile_count,
):
    tile_num = tile_count.shape[0]
    tile_len = observed.shape[1] // tile_num
    obs_grid = observed.reshape(2, tile_num, tile_len)
    slot = lax.broadcasted_iota(jnp.int32, (tile_num, tile_len), 1)
    valid_mask = (slot < tile_count[:, None]).astype(jnp.float32)

    def residuals(camera_block, point_block):
        camera_tile = jnp.take(camera_block, tile_camera, axis=1)[:, :, None]
        point_obs = jnp.take(point_block, point_index, axis=1).reshape(3, tile_num, tile_len)
        return project(camera_tile, point_obs, obs_grid)

    cam_rows, cam_cols = cameras.shape
    pt_rows, pt_cols = points.shape
    n_pt = lax.axis_size("pt")
    n_cam = lax.axis_size("cam")

    def gather_cams(local):
        stacked = lax.all_gather(local, "pt", axis=0)
        return stacked.transpose(1, 0, 2).reshape(cam_rows, n_pt * cam_cols)

    def gather_pts(local):
        flat = local.reshape(pt_rows * pt_cols // 128, 128)
        stacked = lax.all_gather(flat, "cam", axis=0)
        stacked = stacked.reshape(n_cam, pt_rows, pt_cols)
        return stacked.transpose(1, 0, 2).reshape(pt_rows, n_cam * pt_cols)

    def scatter_cams(grad):
        parts = grad.reshape(cam_rows, n_pt, cam_cols).transpose(1, 0, 2)
        return lax.psum_scatter(parts, "pt", scatter_dimension=0, tiled=False)

    def scatter_pts(grad):
        parts = grad.reshape(pt_rows, n_cam, pt_cols).transpose(1, 0, 2)
        parts = parts.reshape(n_cam, pt_rows * pt_cols // 128, 128)
        share = lax.psum_scatter(parts, "cam", scatter_dimension=0, tiled=False)
        return share.reshape(pt_rows, pt_cols)

    camera_block = gather_cams(cameras)
    point_block = gather_pts(points)
    residual, pullback = jax.vjp(residuals, camera_block, point_block)
    cotangent = residual * (reweight(residual) * valid_mask)
    camera_grad, point_grad = pullback(cotangent)
    camera_share = scatter_cams(camera_grad)
    point_share = scatter_pts(point_grad)
    new_cameras, new_cam_first, new_cam_second = adam_step(
        cameras, cam_first, cam_second, camera_share
    )
    new_points, new_pt_first, new_pt_second = adam_step(points, pt_first, pt_second, point_share)
    new_cam_block = gather_cams(new_cameras)
    new_pt_block = gather_pts(new_points)
    final = residuals(new_cam_block, new_pt_block)
    final_weight = (reweight(final) * valid_mask).reshape(-1)
    final_residual = (final * valid_mask).reshape(2, -1)
    return (
        new_cameras,
        new_cam_first,
        new_cam_second,
        new_points,
        new_pt_first,
        new_pt_second,
        final_residual,
        final_weight,
    )


def solution(mesh):
    placed = (
        P(None, ("cam", "pt")),
        P(None, ("cam", "pt")),
        P(None, ("cam", "pt")),
        P(None, ("pt", "cam")),
        P(None, ("pt", "cam")),
        P(None, ("pt", "cam")),
        P(None, ("cam", "pt")),
        P(("cam", "pt")),
        P(("cam", "pt")),
        P(("cam", "pt")),
    )
    return jax.shard_map(
        on_device,
        mesh=mesh,
        in_specs=placed,
        out_specs=(
            P(None, ("cam", "pt")),
            P(None, ("cam", "pt")),
            P(None, ("cam", "pt")),
            P(None, ("pt", "cam")),
            P(None, ("pt", "cam")),
            P(None, ("pt", "cam")),
            P(None, ("cam", "pt")),
            P(("cam", "pt")),
        ),
        check_vma=False,
    )
```

```python
import functools

import jax
import jax.numpy as jnp
from jax import lax
from jax.sharding import PartitionSpec as P
from jax.experimental import pallas as pl
from jax.experimental.pallas import tpu as pltpu

STEP = 10
from jax.experimental import pallas as pl
from jax.experimental.pallas import tpu as pltpu

LANES = 128
SLOT_BLK = 1024


def _split3(x):
    first = x.astype(jnp.bfloat16)
    rest = x - first.astype(jnp.float32)
    second = rest.astype(jnp.bfloat16)
    third = (rest - second.astype(jnp.float32)).astype(jnp.bfloat16)
    return first, second, third


def _gather_kernel(table_ref, index_ref, out_ref, pieces_ref):
    rows = table_ref.shape[0]
    highs = table_ref.shape[1]

    @pl.when(pl.program_id(0) == 0)
    def _():
        first, second, third = _split3(table_ref[...])
        pieces_ref[0:rows, :] = first
        pieces_ref[rows:2 * rows, :] = second
        pieces_ref[2 * rows:3 * rows, :] = third

    index = index_ref[...]
    blk = index.shape[1]
    high = index // LANES
    low = index % LANES
    onehot = (lax.broadcasted_iota(jnp.int32, (highs, blk), 0) == high).astype(jnp.bfloat16)
    picked = jnp.dot(pieces_ref[...], onehot, preferred_element_type=jnp.float32)
    match = lax.broadcasted_iota(jnp.int32, (LANES, blk), 0) == low
    ncoord = rows // LANES
    sums = []
    for g in range(3 * ncoord):
        part = picked[g * LANES:(g + 1) * LANES, :]
        sums.append(jnp.sum(jnp.where(match, part, 0.0), axis=0, keepdims=True))
    for c in range(ncoord):
        out_ref[c:c + 1, :] = sums[c] + sums[ncoord + c] + sums[2 * ncoord + c]


def gather_points(table, index):
    ncoord = table.shape[0] // LANES
    highs = table.shape[1]
    slots = index.shape[0]
    blk = min(SLOT_BLK, slots)
    return pl.pallas_call(
        _gather_kernel,
        grid=(slots // blk,),
        in_specs=[
            pl.BlockSpec((ncoord * LANES, highs), lambda i: (0, 0)),
            pl.BlockSpec((1, blk), lambda i: (0, i)),
        ],
        out_specs=pl.BlockSpec((ncoord, blk), lambda i: (0, i)),
        out_shape=jax.ShapeDtypeStruct((ncoord, slots), jnp.float32),
        scratch_shapes=[pltpu.VMEM((3 * ncoord * LANES, highs), jnp.bfloat16)],
        compiler_params=pltpu.CompilerParams(dimension_semantics=("arbitrary",)),
    )(table, index.reshape(1, slots))


def _scatter_kernel(grad_ref, index_ref, out_ref, acc_ref):
    ncoord, slots = grad_ref.shape
    highs = out_ref.shape[1]
    rows = ncoord * LANES
    blk = min(SLOT_BLK, slots)

    def chunk(step, carry):
        start = pl.multiple_of(step * blk, blk)
        index = index_ref[:, pl.ds(start, blk)]
        high = index // LANES
        low = index % LANES
        onehot = (lax.broadcasted_iota(jnp.int32, (highs, blk), 0) == high).astype(jnp.bfloat16)
        match = lax.broadcasted_iota(jnp.int32, (LANES, blk), 0) == low
        grad = grad_ref[:, pl.ds(start, blk)]
        spread = jnp.concatenate(
            [jnp.where(match, grad[c:c + 1, :], 0.0) for c in range(ncoord)], axis=0
        )
        first, second, third = _split3(spread)
        weights = jnp.concatenate([first, second, third], axis=0)
        acc_ref[...] += lax.dot_general(
            weights, onehot, (((1,), (1,)), ((), ())), preferred_element_type=jnp.float32
        )
        return carry

    acc_ref[...] = jnp.zeros(acc_ref.shape, jnp.float32)
    lax.fori_loop(0, slots // blk, chunk, 0)
    acc = acc_ref[...]
    out_ref[...] = (acc[0:rows] + acc[rows:2 * rows]) + acc[2 * rows:3 * rows]


def scatter_points(grad, index, highs):
    ncoord, slots = grad.shape
    return pl.pallas_call(
        _scatter_kernel,
        out_shape=jax.ShapeDtypeStruct((ncoord * LANES, highs), jnp.float32),
        scratch_shapes=[pltpu.VMEM((3 * ncoord * LANES, highs), jnp.float32)],
    )(grad, index.reshape(1, slots))


@functools.partial(jax.custom_vjp, nondiff_argnums=(2,))
def take_points(table, index, highs):
    return gather_points(table, index)


def _take_fwd(table, index, highs):
    return gather_points(table, index), index


def _take_bwd(highs, index, grad):
    return scatter_points(grad, index, highs), None


take_points.defvjp(_take_fwd, _take_bwd)


def project(camera_tile, point_obs, observed):
    axis_angle = camera_tile[0:3]
    theta_sq = jnp.sum(axis_angle * axis_angle, axis=0)
    sine_term = (
        1.0
        - theta_sq / 6.0
        + theta_sq * theta_sq / 120.0
        - theta_sq * theta_sq * theta_sq / 5040.0
        + theta_sq * theta_sq * theta_sq * theta_sq / 362880.0
    )
    cosine_term = (
        0.5
        - theta_sq / 24.0
        + theta_sq * theta_sq / 720.0
        - theta_sq * theta_sq * theta_sq / 40320.0
        + theta_sq * theta_sq * theta_sq * theta_sq / 3628800.0
    )
    crossed = jnp.stack(
        [
            axis_angle[1] * point_obs[2] - axis_angle[2] * point_obs[1],
            axis_angle[2] * point_obs[0] - axis_angle[0] * point_obs[2],
            axis_angle[0] * point_obs[1] - axis_angle[1] * point_obs[0],
        ]
    )
    inner = jnp.sum(axis_angle * point_obs, axis=0)
    camera_frame = (
        point_obs
        + sine_term * crossed
        + cosine_term * (axis_angle * inner - theta_sq * point_obs)
        + camera_tile[3:6]
    )
    horizontal = camera_frame[0] / camera_frame[2]
    vertical = camera_frame[1] / camera_frame[2]
    radius_sq = horizontal * horizontal + vertical * vertical
    scale_term = camera_tile[6] * (
        1.0 + camera_tile[7] * radius_sq + camera_tile[8] * radius_sq * radius_sq
    )
    return jnp.stack([scale_term * horizontal - observed[0], scale_term * vertical - observed[1]])


def reweight(residual):
    return 1.0 / (1.0 + residual[0] * residual[0] + residual[1] * residual[1])


def adam_step(current, moment_one, moment_two, gradient):
    moment_one = 0.9 * moment_one + 0.1 * gradient
    moment_two = 0.999 * moment_two + 0.001 * gradient * gradient
    corrected_one = moment_one / (1.0 - 0.9**STEP)
    corrected_two = moment_two / (1.0 - 0.999**STEP)
    return (
        current - 0.05 * corrected_one / (jnp.sqrt(corrected_two) + 1e-08),
        moment_one,
        moment_two,
    )


def on_device(
    cameras,
    cam_first,
    cam_second,
    points,
    pt_first,
    pt_second,
    observed,
    tile_camera,
    point_index,
    tile_count,
):
    tile_num = tile_count.shape[0]
    tile_len = observed.shape[1] // tile_num
    obs_grid = observed.reshape(2, tile_num, tile_len)
    slot = lax.broadcasted_iota(jnp.int32, (tile_num, tile_len), 1)
    valid_mask = (slot < tile_count[:, None]).astype(jnp.float32)

    def residuals(camera_block, point_block):
        camera_tile = jnp.take(camera_block, tile_camera, axis=1)[:, :, None]
        point_obs = take_points(point_block, point_index, point_block.shape[1]).reshape(3, tile_num, tile_len)
        return project(camera_tile, point_obs, obs_grid)

    cam_rows, cam_cols = cameras.shape
    pt_rows, pt_cols = points.shape
    n_pt = lax.axis_size("pt")
    n_cam = lax.axis_size("cam")

    def gather_cams(local):
        stacked = lax.all_gather(local, "pt", axis=0)
        return stacked.transpose(1, 0, 2).reshape(cam_rows, n_pt * cam_cols)

    def gather_pts(local):
        flat = local.reshape(pt_rows * pt_cols // LANES, LANES)
        stacked = lax.all_gather(flat, "cam", axis=0)
        stacked = stacked.reshape(n_cam, pt_rows, pt_cols // LANES, LANES)
        return stacked.transpose(1, 3, 0, 2).reshape(pt_rows * LANES, n_cam * pt_cols // LANES)

    def scatter_cams(grad):
        parts = grad.reshape(cam_rows, n_pt, cam_cols).transpose(1, 0, 2)
        return lax.psum_scatter(parts, "pt", scatter_dimension=0, tiled=False)

    def scatter_pts(grad):
        parts = grad.reshape(pt_rows, LANES, n_cam, pt_cols // LANES).transpose(2, 0, 3, 1)
        parts = parts.reshape(n_cam, pt_rows * pt_cols // LANES, LANES)
        share = lax.psum_scatter(parts, "cam", scatter_dimension=0, tiled=False)
        return share.reshape(pt_rows, pt_cols)

    camera_block = gather_cams(cameras)
    point_block = gather_pts(points)
    residual, pullback = jax.vjp(residuals, camera_block, point_block)
    cotangent = residual * (reweight(residual) * valid_mask)
    camera_grad, point_grad = pullback(cotangent)
    camera_share = scatter_cams(camera_grad)
    point_share = scatter_pts(point_grad)
    new_cameras, new_cam_first, new_cam_second = adam_step(
        cameras, cam_first, cam_second, camera_share
    )
    new_points, new_pt_first, new_pt_second = adam_step(points, pt_first, pt_second, point_share)
    new_cam_block = gather_cams(new_cameras)
    new_pt_block = gather_pts(new_points)
    final = residuals(new_cam_block, new_pt_block)
    final_weight = (reweight(final) * valid_mask).reshape(-1)
    final_residual = (final * valid_mask).reshape(2, -1)
    return (
        new_cameras,
        new_cam_first,
        new_cam_second,
        new_points,
        new_pt_first,
        new_pt_second,
        final_residual,
        final_weight,
    )


def solution(mesh):
    placed = (
        P(None, ("cam", "pt")),
        P(None, ("cam", "pt")),
        P(None, ("cam", "pt")),
        P(None, ("pt", "cam")),
        P(None, ("pt", "cam")),
        P(None, ("pt", "cam")),
        P(None, ("cam", "pt")),
        P(("cam", "pt")),
        P(("cam", "pt")),
        P(("cam", "pt")),
    )
    return jax.shard_map(
        on_device,
        mesh=mesh,
        in_specs=placed,
        out_specs=(
            P(None, ("cam", "pt")),
            P(None, ("cam", "pt")),
            P(None, ("cam", "pt")),
            P(None, ("pt", "cam")),
            P(None, ("pt", "cam")),
            P(None, ("pt", "cam")),
            P(None, ("cam", "pt")),
            P(("cam", "pt")),
        ),
        check_vma=False,
    )
```

```python
import functools

import jax
import jax.numpy as jnp
from jax import lax
from jax.sharding import PartitionSpec as P
from jax.experimental import pallas as pl
from jax.experimental.pallas import tpu as pltpu

STEP = 10
from jax.experimental import pallas as pl
from jax.experimental.pallas import tpu as pltpu

LANES = 128
SLOT_BLK = 1024


def _split3(x):
    first = x.astype(jnp.bfloat16)
    rest = x - first.astype(jnp.float32)
    second = rest.astype(jnp.bfloat16)
    third = (rest - second.astype(jnp.float32)).astype(jnp.bfloat16)
    return first, second, third


def _gather_kernel(table_ref, index_ref, out_ref, pieces_ref):
    rows = table_ref.shape[0]
    highs = table_ref.shape[1]

    @pl.when(pl.program_id(0) == 0)
    def _():
        first, second, third = _split3(table_ref[...])
        pieces_ref[0:rows, :] = first
        pieces_ref[rows:2 * rows, :] = second
        pieces_ref[2 * rows:3 * rows, :] = third

    index = index_ref[...]
    blk = index.shape[1]
    high = index // LANES
    low = index % LANES
    onehot = (lax.broadcasted_iota(jnp.int32, (highs, blk), 0) == high).astype(jnp.bfloat16)
    picked = jnp.dot(pieces_ref[...], onehot, preferred_element_type=jnp.float32)
    match = lax.broadcasted_iota(jnp.int32, (LANES, blk), 0) == low
    ncoord = rows // LANES
    sums = []
    for g in range(3 * ncoord):
        part = picked[g * LANES:(g + 1) * LANES, :]
        sums.append(jnp.sum(jnp.where(match, part, 0.0), axis=0, keepdims=True))
    for c in range(ncoord):
        out_ref[c:c + 1, :] = sums[c] + sums[ncoord + c] + sums[2 * ncoord + c]


def gather_points(table, index):
    ncoord = table.shape[0] // LANES
    highs = table.shape[1]
    slots = index.shape[0]
    blk = min(SLOT_BLK, slots)
    return pl.pallas_call(
        _gather_kernel,
        grid=(slots // blk,),
        in_specs=[
            pl.BlockSpec((ncoord * LANES, highs), lambda i: (0, 0)),
            pl.BlockSpec((1, blk), lambda i: (0, i)),
        ],
        out_specs=pl.BlockSpec((ncoord, blk), lambda i: (0, i)),
        out_shape=jax.ShapeDtypeStruct((ncoord, slots), jnp.float32),
        scratch_shapes=[pltpu.VMEM((3 * ncoord * LANES, highs), jnp.bfloat16)],
        compiler_params=pltpu.CompilerParams(dimension_semantics=("arbitrary",)),
    )(table, index.reshape(1, slots))


def _scatter_kernel(grad_ref, index_ref, out_ref, acc_ref):
    ncoord, slots = grad_ref.shape
    highs = out_ref.shape[1]
    rows = ncoord * LANES
    blk = min(SLOT_BLK, slots)

    def chunk(step, carry):
        start = pl.multiple_of(step * blk, blk)
        index = index_ref[:, pl.ds(start, blk)]
        high = index // LANES
        low = index % LANES
        onehot = (lax.broadcasted_iota(jnp.int32, (highs, blk), 0) == high).astype(jnp.bfloat16)
        match = lax.broadcasted_iota(jnp.int32, (LANES, blk), 0) == low
        grad = grad_ref[:, pl.ds(start, blk)]
        spread = jnp.concatenate(
            [jnp.where(match, grad[c:c + 1, :], 0.0) for c in range(ncoord)], axis=0
        )
        first, second, third = _split3(spread)
        weights = jnp.concatenate([first, second, third], axis=0)
        acc_ref[...] += lax.dot_general(
            weights, onehot, (((1,), (1,)), ((), ())), preferred_element_type=jnp.float32
        )
        return carry

    acc_ref[...] = jnp.zeros(acc_ref.shape, jnp.float32)
    lax.fori_loop(0, slots // blk, chunk, 0)
    acc = acc_ref[...]
    out_ref[...] = (acc[0:rows] + acc[rows:2 * rows]) + acc[2 * rows:3 * rows]


def scatter_points(grad, index, highs):
    ncoord, slots = grad.shape
    return pl.pallas_call(
        _scatter_kernel,
        out_shape=jax.ShapeDtypeStruct((ncoord * LANES, highs), jnp.float32),
        scratch_shapes=[pltpu.VMEM((3 * ncoord * LANES, highs), jnp.float32)],
    )(grad, index.reshape(1, slots))


@functools.partial(jax.custom_vjp, nondiff_argnums=(2,))
def take_points(table, index, highs):
    return gather_points(table, index)


def _take_fwd(table, index, highs):
    return gather_points(table, index), index


def _take_bwd(highs, index, grad):
    return scatter_points(grad, index, highs), None


take_points.defvjp(_take_fwd, _take_bwd)


def project(camera_tile, point_obs, observed):
    axis_angle = camera_tile[0:3]
    theta_sq = jnp.sum(axis_angle * axis_angle, axis=0)
    sine_term = (
        1.0
        - theta_sq / 6.0
        + theta_sq * theta_sq / 120.0
        - theta_sq * theta_sq * theta_sq / 5040.0
        + theta_sq * theta_sq * theta_sq * theta_sq / 362880.0
    )
    cosine_term = (
        0.5
        - theta_sq / 24.0
        + theta_sq * theta_sq / 720.0
        - theta_sq * theta_sq * theta_sq / 40320.0
        + theta_sq * theta_sq * theta_sq * theta_sq / 3628800.0
    )
    crossed = jnp.stack(
        [
            axis_angle[1] * point_obs[2] - axis_angle[2] * point_obs[1],
            axis_angle[2] * point_obs[0] - axis_angle[0] * point_obs[2],
            axis_angle[0] * point_obs[1] - axis_angle[1] * point_obs[0],
        ]
    )
    inner = jnp.sum(axis_angle * point_obs, axis=0)
    camera_frame = (
        point_obs
        + sine_term * crossed
        + cosine_term * (axis_angle * inner - theta_sq * point_obs)
        + camera_tile[3:6]
    )
    horizontal = camera_frame[0] / camera_frame[2]
    vertical = camera_frame[1] / camera_frame[2]
    radius_sq = horizontal * horizontal + vertical * vertical
    scale_term = camera_tile[6] * (
        1.0 + camera_tile[7] * radius_sq + camera_tile[8] * radius_sq * radius_sq
    )
    return jnp.stack([scale_term * horizontal - observed[0], scale_term * vertical - observed[1]])


def reweight(residual):
    return 1.0 / (1.0 + residual[0] * residual[0] + residual[1] * residual[1])


def adam_step(current, moment_one, moment_two, gradient):
    moment_one = 0.9 * moment_one + 0.1 * gradient
    moment_two = 0.999 * moment_two + 0.001 * gradient * gradient
    corrected_one = moment_one / (1.0 - 0.9**STEP)
    corrected_two = moment_two / (1.0 - 0.999**STEP)
    return (
        current - 0.05 * corrected_one / (jnp.sqrt(corrected_two) + 1e-08),
        moment_one,
        moment_two,
    )


def on_device(
    cameras,
    cam_first,
    cam_second,
    points,
    pt_first,
    pt_second,
    observed,
    tile_camera,
    point_index,
    tile_count,
):
    tile_num = tile_count.shape[0]
    tile_len = observed.shape[1] // tile_num
    obs_grid = observed.reshape(2, tile_num, tile_len)
    slot = lax.broadcasted_iota(jnp.int32, (tile_num, tile_len), 1)
    valid_mask = (slot < tile_count[:, None]).astype(jnp.float32)

    def residuals(camera_block, point_block):
        camera_tile = jnp.take(camera_block, tile_camera, axis=1)[:, :, None]
        point_obs = take_points(point_block, point_index, point_block.shape[1]).reshape(3, tile_num, tile_len)
        return project(camera_tile, point_obs, obs_grid)

    cam_rows, cam_cols = cameras.shape
    pt_rows, pt_cols = points.shape
    n_pt = lax.axis_size("pt")
    n_cam = lax.axis_size("cam")

    def doubling_gather(local, axis_name, size):
        me = lax.axis_index(axis_name)
        buf = local[None]
        dist = 1
        while dist < size:
            pairs = [(i, i ^ dist) for i in range(size)]
            other = lax.ppermute(buf, axis_name, pairs)
            low_half = (me // dist) % 2 == 0
            buf = jnp.where(
                low_half,
                jnp.concatenate([buf, other], axis=0),
                jnp.concatenate([other, buf], axis=0),
            )
            dist *= 2
        return buf

    def halving_scatter(parts, axis_name, size):
        me = lax.axis_index(axis_name)
        buf = parts
        dist = size // 2
        while dist >= 1:
            pairs = [(i, i ^ dist) for i in range(size)]
            low_half = (me // dist) % 2 == 0
            half = buf.shape[0] // 2
            first, second = buf[:half], buf[half:]
            keep = jnp.where(low_half, first, second)
            send = jnp.where(low_half, second, first)
            buf = keep + lax.ppermute(send, axis_name, pairs)
            dist //= 2
        return buf[0]

    def gather_cams(local):
        stacked = doubling_gather(local, "pt", n_pt)
        return stacked.transpose(1, 0, 2).reshape(cam_rows, n_pt * cam_cols)

    def gather_pts(local):
        flat = local.reshape(pt_rows * pt_cols // LANES, LANES)
        stacked = doubling_gather(flat, "cam", n_cam)
        stacked = stacked.reshape(n_cam, pt_rows, pt_cols // LANES, LANES)
        return stacked.transpose(1, 3, 0, 2).reshape(pt_rows * LANES, n_cam * pt_cols // LANES)

    def scatter_cams(grad):
        parts = grad.reshape(cam_rows, n_pt, cam_cols).transpose(1, 0, 2)
        return halving_scatter(parts, "pt", n_pt)

    def scatter_pts(grad):
        parts = grad.reshape(pt_rows, LANES, n_cam, pt_cols // LANES).transpose(2, 0, 3, 1)
        parts = parts.reshape(n_cam, pt_rows * pt_cols // LANES, LANES)
        share = halving_scatter(parts, "cam", n_cam)
        return share.reshape(pt_rows, pt_cols)

    camera_block = gather_cams(cameras)
    point_block = gather_pts(points)
    residual, pullback = jax.vjp(residuals, camera_block, point_block)
    cotangent = residual * (reweight(residual) * valid_mask)
    camera_grad, point_grad = pullback(cotangent)
    camera_share = scatter_cams(camera_grad)
    point_share = scatter_pts(point_grad)
    new_cameras, new_cam_first, new_cam_second = adam_step(
        cameras, cam_first, cam_second, camera_share
    )
    new_points, new_pt_first, new_pt_second = adam_step(points, pt_first, pt_second, point_share)
    new_cam_block = gather_cams(new_cameras)
    new_pt_block = gather_pts(new_points)
    final = residuals(new_cam_block, new_pt_block)
    final_weight = (reweight(final) * valid_mask).reshape(-1)
    final_residual = (final * valid_mask).reshape(2, -1)
    return (
        new_cameras,
        new_cam_first,
        new_cam_second,
        new_points,
        new_pt_first,
        new_pt_second,
        final_residual,
        final_weight,
    )


def solution(mesh):
    placed = (
        P(None, ("cam", "pt")),
        P(None, ("cam", "pt")),
        P(None, ("cam", "pt")),
        P(None, ("pt", "cam")),
        P(None, ("pt", "cam")),
        P(None, ("pt", "cam")),
        P(None, ("cam", "pt")),
        P(("cam", "pt")),
        P(("cam", "pt")),
        P(("cam", "pt")),
    )
    return jax.shard_map(
        on_device,
        mesh=mesh,
        in_specs=placed,
        out_specs=(
            P(None, ("cam", "pt")),
            P(None, ("cam", "pt")),
            P(None, ("cam", "pt")),
            P(None, ("pt", "cam")),
            P(None, ("pt", "cam")),
            P(None, ("pt", "cam")),
            P(None, ("cam", "pt")),
            P(("cam", "pt")),
        ),
        check_vma=False,
    )
```

```python
import functools

import jax
import jax.numpy as jnp
from jax import lax
from jax.sharding import PartitionSpec as P
from jax.experimental import pallas as pl
from jax.experimental.pallas import tpu as pltpu

STEP = 10
from jax.experimental import pallas as pl
from jax.experimental.pallas import tpu as pltpu

LANES = 128
SLOT_BLK = 1024


def _split3(x):
    first = x.astype(jnp.bfloat16)
    rest = x - first.astype(jnp.float32)
    second = rest.astype(jnp.bfloat16)
    third = (rest - second.astype(jnp.float32)).astype(jnp.bfloat16)
    return first, second, third


def _gather_kernel(table_ref, index_ref, out_ref, pieces_ref):
    rows = table_ref.shape[0]
    highs = table_ref.shape[1]

    @pl.when(pl.program_id(0) == 0)
    def _():
        first, second, third = _split3(table_ref[...])
        pieces_ref[0:rows, :] = first
        pieces_ref[rows:2 * rows, :] = second
        pieces_ref[2 * rows:3 * rows, :] = third

    index = index_ref[...]
    blk = index.shape[1]
    high = index // LANES
    low = index % LANES
    onehot = (lax.broadcasted_iota(jnp.int32, (highs, blk), 0) == high).astype(jnp.bfloat16)
    picked = jnp.dot(pieces_ref[...], onehot, preferred_element_type=jnp.float32)
    match = lax.broadcasted_iota(jnp.int32, (LANES, blk), 0) == low
    ncoord = rows // LANES
    sums = []
    for g in range(3 * ncoord):
        part = picked[g * LANES:(g + 1) * LANES, :]
        sums.append(jnp.sum(jnp.where(match, part, 0.0), axis=0, keepdims=True))
    for c in range(ncoord):
        out_ref[c:c + 1, :] = sums[c] + sums[ncoord + c] + sums[2 * ncoord + c]


def gather_points(table, index):
    ncoord = table.shape[0] // LANES
    highs = table.shape[1]
    slots = index.shape[0]
    blk = min(SLOT_BLK, slots)
    return pl.pallas_call(
        _gather_kernel,
        grid=(slots // blk,),
        in_specs=[
            pl.BlockSpec((ncoord * LANES, highs), lambda i: (0, 0)),
            pl.BlockSpec((1, blk), lambda i: (0, i)),
        ],
        out_specs=pl.BlockSpec((ncoord, blk), lambda i: (0, i)),
        out_shape=jax.ShapeDtypeStruct((ncoord, slots), jnp.float32),
        scratch_shapes=[pltpu.VMEM((3 * ncoord * LANES, highs), jnp.bfloat16)],
        compiler_params=pltpu.CompilerParams(dimension_semantics=("arbitrary",)),
    )(table, index.reshape(1, slots))


def _scatter_kernel(grad_ref, index_ref, out_ref, acc_ref):
    ncoord, slots = grad_ref.shape
    highs = out_ref.shape[1]
    rows = ncoord * LANES
    blk = min(SLOT_BLK, slots)

    def chunk(step, carry):
        start = pl.multiple_of(step * blk, blk)
        index = index_ref[:, pl.ds(start, blk)]
        high = index // LANES
        low = index % LANES
        onehot = (lax.broadcasted_iota(jnp.int32, (highs, blk), 0) == high).astype(jnp.bfloat16)
        match = lax.broadcasted_iota(jnp.int32, (LANES, blk), 0) == low
        grad = grad_ref[:, pl.ds(start, blk)]
        spread = jnp.concatenate(
            [jnp.where(match, grad[c:c + 1, :], 0.0) for c in range(ncoord)], axis=0
        )
        first, second, third = _split3(spread)
        weights = jnp.concatenate([first, second, third], axis=0)
        acc_ref[...] += lax.dot_general(
            weights, onehot, (((1,), (1,)), ((), ())), preferred_element_type=jnp.float32
        )
        return carry

    acc_ref[...] = jnp.zeros(acc_ref.shape, jnp.float32)
    lax.fori_loop(0, slots // blk, chunk, 0)
    acc = acc_ref[...]
    out_ref[...] = (acc[0:rows] + acc[rows:2 * rows]) + acc[2 * rows:3 * rows]


def scatter_points(grad, index, highs):
    ncoord, slots = grad.shape
    return pl.pallas_call(
        _scatter_kernel,
        out_shape=jax.ShapeDtypeStruct((ncoord * LANES, highs), jnp.float32),
        scratch_shapes=[pltpu.VMEM((3 * ncoord * LANES, highs), jnp.float32)],
    )(grad, index.reshape(1, slots))


@functools.partial(jax.custom_vjp, nondiff_argnums=(2,))
def take_points(table, index, highs):
    return gather_points(table, index)


def _take_fwd(table, index, highs):
    return gather_points(table, index), index


def _take_bwd(highs, index, grad):
    return scatter_points(grad, index, highs), None


take_points.defvjp(_take_fwd, _take_bwd)


def project(camera_tile, point_obs, observed):
    axis_angle = camera_tile[0:3]
    theta_sq = jnp.sum(axis_angle * axis_angle, axis=0)
    sine_term = (
        1.0
        - theta_sq / 6.0
        + theta_sq * theta_sq / 120.0
        - theta_sq * theta_sq * theta_sq / 5040.0
        + theta_sq * theta_sq * theta_sq * theta_sq / 362880.0
    )
    cosine_term = (
        0.5
        - theta_sq / 24.0
        + theta_sq * theta_sq / 720.0
        - theta_sq * theta_sq * theta_sq / 40320.0
        + theta_sq * theta_sq * theta_sq * theta_sq / 3628800.0
    )
    crossed = jnp.stack(
        [
            axis_angle[1] * point_obs[2] - axis_angle[2] * point_obs[1],
            axis_angle[2] * point_obs[0] - axis_angle[0] * point_obs[2],
            axis_angle[0] * point_obs[1] - axis_angle[1] * point_obs[0],
        ]
    )
    inner = jnp.sum(axis_angle * point_obs, axis=0)
    camera_frame = (
        point_obs
        + sine_term * crossed
        + cosine_term * (axis_angle * inner - theta_sq * point_obs)
        + camera_tile[3:6]
    )
    horizontal = camera_frame[0] / camera_frame[2]
    vertical = camera_frame[1] / camera_frame[2]
    radius_sq = horizontal * horizontal + vertical * vertical
    scale_term = camera_tile[6] * (
        1.0 + camera_tile[7] * radius_sq + camera_tile[8] * radius_sq * radius_sq
    )
    return jnp.stack([scale_term * horizontal - observed[0], scale_term * vertical - observed[1]])


def reweight(residual):
    return 1.0 / (1.0 + residual[0] * residual[0] + residual[1] * residual[1])


def adam_step(current, moment_one, moment_two, gradient):
    moment_one = 0.9 * moment_one + 0.1 * gradient
    moment_two = 0.999 * moment_two + 0.001 * gradient * gradient
    corrected_one = moment_one / (1.0 - 0.9**STEP)
    corrected_two = moment_two / (1.0 - 0.999**STEP)
    return (
        current - 0.05 * corrected_one / (jnp.sqrt(corrected_two) + 1e-08),
        moment_one,
        moment_two,
    )


def on_device(
    cameras,
    cam_first,
    cam_second,
    points,
    pt_first,
    pt_second,
    observed,
    tile_camera,
    point_index,
    tile_count,
):
    tile_num = tile_count.shape[0]
    tile_len = observed.shape[1] // tile_num
    obs_grid = observed.reshape(2, tile_num, tile_len)
    slot = lax.broadcasted_iota(jnp.int32, (tile_num, tile_len), 1)
    valid_mask = (slot < tile_count[:, None]).astype(jnp.float32)

    def residuals(camera_block, point_block):
        camera_tile = jnp.take(camera_block, tile_camera, axis=1)[:, :, None]
        point_obs = take_points(point_block, point_index, point_block.shape[1]).reshape(3, tile_num, tile_len)
        return project(camera_tile, point_obs, obs_grid)

    cam_rows, cam_cols = cameras.shape
    pt_rows, pt_cols = points.shape
    n_pt = lax.axis_size("pt")
    n_cam = lax.axis_size("cam")

    def doubling_gather(local, axis_name, size):
        me = lax.axis_index(axis_name)
        buf = local[None]
        dist = 1
        while dist < size:
            pairs = [(i, i ^ dist) for i in range(size)]
            other = lax.ppermute(buf, axis_name, pairs)
            low_half = (me // dist) % 2 == 0
            buf = jnp.where(
                low_half,
                jnp.concatenate([buf, other], axis=0),
                jnp.concatenate([other, buf], axis=0),
            )
            dist *= 2
        return buf

    def butterfly_sum(value, axis_name, size):
        dist = 1
        while dist < size:
            pairs = [(i, i ^ dist) for i in range(size)]
            value = value + lax.ppermute(value, axis_name, pairs)
            dist *= 2
        return value

    def gather_pts(local):
        flat = local.reshape(pt_rows * pt_cols // LANES, LANES)
        stacked = doubling_gather(flat, "cam", n_cam)
        stacked = stacked.reshape(n_cam, pt_rows, pt_cols // LANES, LANES)
        return stacked.transpose(1, 3, 0, 2).reshape(pt_rows * LANES, n_cam * pt_cols // LANES)

    def own_pts(table):
        parts = table.reshape(pt_rows, LANES, n_cam, pt_cols // LANES)
        mine = lax.dynamic_index_in_dim(parts, lax.axis_index("cam"), axis=2, keepdims=False)
        return mine.transpose(0, 2, 1).reshape(pt_rows, pt_cols)

    def own_cams(block):
        start = lax.axis_index("pt") * cam_cols
        return lax.dynamic_slice_in_dim(block, start, cam_cols, axis=1)

    cam_state = jnp.concatenate([cameras, cam_first, cam_second], axis=0)
    cam_state = doubling_gather(cam_state, "pt", n_pt)
    cam_state = cam_state.transpose(1, 0, 2).reshape(3, cam_rows, n_pt * cam_cols)
    camera_block, first_block, second_block = cam_state[0], cam_state[1], cam_state[2]
    point_block = gather_pts(points)
    residual, pullback = jax.vjp(residuals, camera_block, point_block)
    cotangent = residual * (reweight(residual) * valid_mask)
    camera_grad, point_grad = pullback(cotangent)
    camera_grad = butterfly_sum(
        camera_grad.reshape(cam_rows * n_pt, cam_cols), "pt", n_pt
    ).reshape(cam_rows, n_pt * cam_cols)
    point_grad = butterfly_sum(point_grad, "cam", n_cam)
    new_cam_block, new_cam_first, new_cam_second = adam_step(
        camera_block, first_block, second_block, camera_grad
    )
    new_pt_block, new_pt_first, new_pt_second = adam_step(
        point_block, gather_pts(pt_first), gather_pts(pt_second), point_grad
    )
    new_cameras = own_cams(new_cam_block)
    new_cam_first = own_cams(new_cam_first)
    new_cam_second = own_cams(new_cam_second)
    new_points = own_pts(new_pt_block)
    new_pt_first = own_pts(new_pt_first)
    new_pt_second = own_pts(new_pt_second)
    final = residuals(new_cam_block, new_pt_block)
    final_weight = (reweight(final) * valid_mask).reshape(-1)
    final_residual = (final * valid_mask).reshape(2, -1)
    return (
        new_cameras,
        new_cam_first,
        new_cam_second,
        new_points,
        new_pt_first,
        new_pt_second,
        final_residual,
        final_weight,
    )


def solution(mesh):
    placed = (
        P(None, ("cam", "pt")),
        P(None, ("cam", "pt")),
        P(None, ("cam", "pt")),
        P(None, ("pt", "cam")),
        P(None, ("pt", "cam")),
        P(None, ("pt", "cam")),
        P(None, ("cam", "pt")),
        P(("cam", "pt")),
        P(("cam", "pt")),
        P(("cam", "pt")),
    )
    return jax.shard_map(
        on_device,
        mesh=mesh,
        in_specs=placed,
        out_specs=(
            P(None, ("cam", "pt")),
            P(None, ("cam", "pt")),
            P(None, ("cam", "pt")),
            P(None, ("pt", "cam")),
            P(None, ("pt", "cam")),
            P(None, ("pt", "cam")),
            P(None, ("cam", "pt")),
            P(("cam", "pt")),
        ),
        check_vma=False,
    )
```

```python
import functools

import jax
import jax.numpy as jnp
from jax import lax
from jax.sharding import PartitionSpec as P
from jax.experimental import pallas as pl
from jax.experimental.pallas import tpu as pltpu

STEP = 10
from jax.experimental import pallas as pl
from jax.experimental.pallas import tpu as pltpu

LANES = 128
SLOT_BLK = 1024


def _split3(x):
    first = x.astype(jnp.bfloat16)
    rest = x - first.astype(jnp.float32)
    second = rest.astype(jnp.bfloat16)
    third = (rest - second.astype(jnp.float32)).astype(jnp.bfloat16)
    return first, second, third


def _gather_kernel(table_ref, index_ref, out_ref, pieces_ref):
    rows = table_ref.shape[0]
    highs = table_ref.shape[1]

    @pl.when(pl.program_id(0) == 0)
    def _():
        first, second, third = _split3(table_ref[...])
        pieces_ref[0:rows, :] = first
        pieces_ref[rows:2 * rows, :] = second
        pieces_ref[2 * rows:3 * rows, :] = third

    index = index_ref[...]
    blk = index.shape[1]
    high = index // LANES
    low = index % LANES
    onehot = (lax.broadcasted_iota(jnp.int32, (highs, blk), 0) == high).astype(jnp.bfloat16)
    picked = jnp.dot(pieces_ref[...], onehot, preferred_element_type=jnp.float32)
    match = lax.broadcasted_iota(jnp.int32, (LANES, blk), 0) == low
    ncoord = rows // LANES
    sums = []
    for g in range(3 * ncoord):
        part = picked[g * LANES:(g + 1) * LANES, :]
        sums.append(jnp.sum(jnp.where(match, part, 0.0), axis=0, keepdims=True))
    for c in range(ncoord):
        out_ref[c:c + 1, :] = sums[c] + sums[ncoord + c] + sums[2 * ncoord + c]


def gather_points(table, index):
    ncoord = table.shape[0] // LANES
    highs = table.shape[1]
    slots = index.shape[0]
    blk = min(SLOT_BLK, slots)
    return pl.pallas_call(
        _gather_kernel,
        grid=(slots // blk,),
        in_specs=[
            pl.BlockSpec((ncoord * LANES, highs), lambda i: (0, 0)),
            pl.BlockSpec((1, blk), lambda i: (0, i)),
        ],
        out_specs=pl.BlockSpec((ncoord, blk), lambda i: (0, i)),
        out_shape=jax.ShapeDtypeStruct((ncoord, slots), jnp.float32),
        scratch_shapes=[pltpu.VMEM((3 * ncoord * LANES, highs), jnp.bfloat16)],
        compiler_params=pltpu.CompilerParams(dimension_semantics=("arbitrary",)),
    )(table, index.reshape(1, slots))


def _scatter_kernel(grad_ref, index_ref, out_ref, acc_ref):
    ncoord, slots = grad_ref.shape
    highs = out_ref.shape[1]
    rows = ncoord * LANES
    blk = min(SLOT_BLK, slots)

    def chunk(step, carry):
        start = pl.multiple_of(step * blk, blk)
        index = index_ref[:, pl.ds(start, blk)]
        high = index // LANES
        low = index % LANES
        onehot = (lax.broadcasted_iota(jnp.int32, (highs, blk), 0) == high).astype(jnp.bfloat16)
        match = lax.broadcasted_iota(jnp.int32, (LANES, blk), 0) == low
        grad = grad_ref[:, pl.ds(start, blk)]
        spread = jnp.concatenate(
            [jnp.where(match, grad[c:c + 1, :], 0.0) for c in range(ncoord)], axis=0
        )
        first, second, third = _split3(spread)
        weights = jnp.concatenate([first, second, third], axis=0)
        acc_ref[...] += lax.dot_general(
            weights, onehot, (((1,), (1,)), ((), ())), preferred_element_type=jnp.float32
        )
        return carry

    acc_ref[...] = jnp.zeros(acc_ref.shape, jnp.float32)
    lax.fori_loop(0, slots // blk, chunk, 0)
    acc = acc_ref[...]
    out_ref[...] = (acc[0:rows] + acc[rows:2 * rows]) + acc[2 * rows:3 * rows]


def scatter_points(grad, index, highs):
    ncoord, slots = grad.shape
    return pl.pallas_call(
        _scatter_kernel,
        out_shape=jax.ShapeDtypeStruct((ncoord * LANES, highs), jnp.float32),
        scratch_shapes=[pltpu.VMEM((3 * ncoord * LANES, highs), jnp.float32)],
    )(grad, index.reshape(1, slots))


@functools.partial(jax.custom_vjp, nondiff_argnums=(2,))
def take_points(table, index, highs):
    return gather_points(table, index)


def _take_fwd(table, index, highs):
    return gather_points(table, index), index


def _take_bwd(highs, index, grad):
    return scatter_points(grad, index, highs), None


take_points.defvjp(_take_fwd, _take_bwd)


def project(camera_tile, point_obs, observed):
    axis_angle = camera_tile[0:3]
    theta_sq = jnp.sum(axis_angle * axis_angle, axis=0)
    sine_term = (
        1.0
        - theta_sq / 6.0
        + theta_sq * theta_sq / 120.0
        - theta_sq * theta_sq * theta_sq / 5040.0
        + theta_sq * theta_sq * theta_sq * theta_sq / 362880.0
    )
    cosine_term = (
        0.5
        - theta_sq / 24.0
        + theta_sq * theta_sq / 720.0
        - theta_sq * theta_sq * theta_sq / 40320.0
        + theta_sq * theta_sq * theta_sq * theta_sq / 3628800.0
    )
    crossed = jnp.stack(
        [
            axis_angle[1] * point_obs[2] - axis_angle[2] * point_obs[1],
            axis_angle[2] * point_obs[0] - axis_angle[0] * point_obs[2],
            axis_angle[0] * point_obs[1] - axis_angle[1] * point_obs[0],
        ]
    )
    inner = jnp.sum(axis_angle * point_obs, axis=0)
    camera_frame = (
        point_obs
        + sine_term * crossed
        + cosine_term * (axis_angle * inner - theta_sq * point_obs)
        + camera_tile[3:6]
    )
    horizontal = camera_frame[0] / camera_frame[2]
    vertical = camera_frame[1] / camera_frame[2]
    radius_sq = horizontal * horizontal + vertical * vertical
    scale_term = camera_tile[6] * (
        1.0 + camera_tile[7] * radius_sq + camera_tile[8] * radius_sq * radius_sq
    )
    return jnp.stack([scale_term * horizontal - observed[0], scale_term * vertical - observed[1]])


def reweight(residual):
    return 1.0 / (1.0 + residual[0] * residual[0] + residual[1] * residual[1])


def adam_step(current, moment_one, moment_two, gradient):
    moment_one = 0.9 * moment_one + 0.1 * gradient
    moment_two = 0.999 * moment_two + 0.001 * gradient * gradient
    corrected_one = moment_one / (1.0 - 0.9**STEP)
    corrected_two = moment_two / (1.0 - 0.999**STEP)
    return (
        current - 0.05 * corrected_one / (jnp.sqrt(corrected_two) + 1e-08),
        moment_one,
        moment_two,
    )


def on_device(
    cameras,
    cam_first,
    cam_second,
    points,
    pt_first,
    pt_second,
    observed,
    tile_camera,
    point_index,
    tile_count,
):
    tile_num = tile_count.shape[0]
    tile_len = observed.shape[1] // tile_num
    obs_grid = observed.reshape(2, tile_num, tile_len)
    slot = lax.broadcasted_iota(jnp.int32, (tile_num, tile_len), 1)
    valid_mask = (slot < tile_count[:, None]).astype(jnp.float32)

    def residuals(camera_block, point_block):
        camera_tile = jnp.take(camera_block, tile_camera, axis=1)[:, :, None]
        point_obs = take_points(point_block, point_index, point_block.shape[1]).reshape(3, tile_num, tile_len)
        return project(camera_tile, point_obs, obs_grid)

    cam_rows, cam_cols = cameras.shape
    pt_rows, pt_cols = points.shape
    n_pt = lax.axis_size("pt")
    n_cam = lax.axis_size("cam")

    def rounds(size):
        plan = []
        dist = 1
        while dist < size:
            radix = 4 if (size // dist) % 4 == 0 else 2
            plan.append((dist, radix))
            dist *= radix
        return plan

    def partners(size, dist, radix, offset):
        return [
            (i, i + ((((i // dist) % radix) ^ offset) - (i // dist) % radix) * dist)
            for i in range(size)
        ]

    def doubling_gather(local, axis_name, size):
        me = lax.axis_index(axis_name)
        buf = local[None]
        for dist, radix in rounds(size):
            digit = (me // dist) % radix
            got = [buf] + [
                lax.ppermute(buf, axis_name, partners(size, dist, radix, k))
                for k in range(1, radix)
            ]
            stacked = jnp.stack(got)
            buf = jnp.concatenate(
                [
                    lax.dynamic_index_in_dim(stacked, digit ^ p, 0, keepdims=False)
                    for p in range(radix)
                ],
                axis=0,
            )
        return buf

    def butterfly_sum(value, axis_name, size):
        for dist, radix in rounds(size):
            got = [
                lax.ppermute(value, axis_name, partners(size, dist, radix, k))
                for k in range(1, radix)
            ]
            for other in got:
                value = value + other
        return value

    def gather_pts(local):
        flat = local.reshape(pt_rows * pt_cols // LANES, LANES)
        stacked = doubling_gather(flat, "cam", n_cam)
        stacked = stacked.reshape(n_cam, pt_rows, pt_cols // LANES, LANES)
        return stacked.transpose(1, 3, 0, 2).reshape(pt_rows * LANES, n_cam * pt_cols // LANES)

    def own_pts(table):
        parts = table.reshape(pt_rows, LANES, n_cam, pt_cols // LANES)
        mine = lax.dynamic_index_in_dim(parts, lax.axis_index("cam"), axis=2, keepdims=False)
        return mine.transpose(0, 2, 1).reshape(pt_rows, pt_cols)

    def own_cams(block):
        start = lax.axis_index("pt") * cam_cols
        return lax.dynamic_slice_in_dim(block, start, cam_cols, axis=1)

    cam_state = jnp.concatenate([cameras, cam_first, cam_second], axis=0)
    cam_state = doubling_gather(cam_state, "pt", n_pt)
    cam_state = cam_state.transpose(1, 0, 2).reshape(3, cam_rows, n_pt * cam_cols)
    camera_block, first_block, second_block = cam_state[0], cam_state[1], cam_state[2]
    point_block = gather_pts(points)
    residual, pullback = jax.vjp(residuals, camera_block, point_block)
    cotangent = residual * (reweight(residual) * valid_mask)
    camera_grad, point_grad = pullback(cotangent)
    camera_grad = butterfly_sum(
        camera_grad.reshape(cam_rows * n_pt, cam_cols), "pt", n_pt
    ).reshape(cam_rows, n_pt * cam_cols)
    point_grad = butterfly_sum(point_grad, "cam", n_cam)
    new_cam_block, new_cam_first, new_cam_second = adam_step(
        camera_block, first_block, second_block, camera_grad
    )
    new_pt_block, new_pt_first, new_pt_second = adam_step(
        point_block, gather_pts(pt_first), gather_pts(pt_second), point_grad
    )
    new_cameras = own_cams(new_cam_block)
    new_cam_first = own_cams(new_cam_first)
    new_cam_second = own_cams(new_cam_second)
    new_points = own_pts(new_pt_block)
    new_pt_first = own_pts(new_pt_first)
    new_pt_second = own_pts(new_pt_second)
    final = residuals(new_cam_block, new_pt_block)
    final_weight = (reweight(final) * valid_mask).reshape(-1)
    final_residual = (final * valid_mask).reshape(2, -1)
    return (
        new_cameras,
        new_cam_first,
        new_cam_second,
        new_points,
        new_pt_first,
        new_pt_second,
        final_residual,
        final_weight,
    )


def solution(mesh):
    placed = (
        P(None, ("cam", "pt")),
        P(None, ("cam", "pt")),
        P(None, ("cam", "pt")),
        P(None, ("pt", "cam")),
        P(None, ("pt", "cam")),
        P(None, ("pt", "cam")),
        P(None, ("cam", "pt")),
        P(("cam", "pt")),
        P(("cam", "pt")),
        P(("cam", "pt")),
    )
    return jax.shard_map(
        on_device,
        mesh=mesh,
        in_specs=placed,
        out_specs=(
            P(None, ("cam", "pt")),
            P(None, ("cam", "pt")),
            P(None, ("cam", "pt")),
            P(None, ("pt", "cam")),
            P(None, ("pt", "cam")),
            P(None, ("pt", "cam")),
            P(None, ("cam", "pt")),
            P(("cam", "pt")),
        ),
        check_vma=False,
    )
```

```python
import functools

import jax
import jax.numpy as jnp
from jax import lax
from jax.sharding import PartitionSpec as P
from jax.experimental import pallas as pl
from jax.experimental.pallas import tpu as pltpu

STEP = 10
from jax.experimental import pallas as pl
from jax.experimental.pallas import tpu as pltpu

LANES = 128
SLOT_BLK = 1024


def _split3(x):
    first = x.astype(jnp.bfloat16)
    rest = x - first.astype(jnp.float32)
    second = rest.astype(jnp.bfloat16)
    third = (rest - second.astype(jnp.float32)).astype(jnp.bfloat16)
    return first, second, third


def _gather_kernel(table_ref, index_ref, out_ref, pieces_ref):
    rows = table_ref.shape[0]
    highs = table_ref.shape[1]

    @pl.when(pl.program_id(0) == 0)
    def _():
        first, second, third = _split3(table_ref[...])
        pieces_ref[0:rows, :] = first
        pieces_ref[rows:2 * rows, :] = second
        pieces_ref[2 * rows:3 * rows, :] = third

    index = index_ref[...]
    blk = index.shape[1]
    high = index // LANES
    low = index % LANES
    onehot = (lax.broadcasted_iota(jnp.int32, (highs, blk), 0) == high).astype(jnp.bfloat16)
    picked = jnp.dot(pieces_ref[...], onehot, preferred_element_type=jnp.float32)
    match = lax.broadcasted_iota(jnp.int32, (LANES, blk), 0) == low
    ncoord = rows // LANES
    sums = []
    for g in range(3 * ncoord):
        part = picked[g * LANES:(g + 1) * LANES, :]
        sums.append(jnp.sum(jnp.where(match, part, 0.0), axis=0, keepdims=True))
    for c in range(ncoord):
        out_ref[c:c + 1, :] = sums[c] + sums[ncoord + c] + sums[2 * ncoord + c]


def gather_points(table, index):
    ncoord = table.shape[0] // LANES
    highs = table.shape[1]
    slots = index.shape[0]
    blk = min(SLOT_BLK, slots)
    return pl.pallas_call(
        _gather_kernel,
        grid=(slots // blk,),
        in_specs=[
            pl.BlockSpec((ncoord * LANES, highs), lambda i: (0, 0)),
            pl.BlockSpec((1, blk), lambda i: (0, i)),
        ],
        out_specs=pl.BlockSpec((ncoord, blk), lambda i: (0, i)),
        out_shape=jax.ShapeDtypeStruct((ncoord, slots), jnp.float32),
        scratch_shapes=[pltpu.VMEM((3 * ncoord * LANES, highs), jnp.bfloat16)],
        compiler_params=pltpu.CompilerParams(dimension_semantics=("arbitrary",)),
    )(table, index.reshape(1, slots))


def _scatter_kernel(grad_ref, index_ref, out_ref, acc_ref):
    ncoord, slots = grad_ref.shape
    highs = out_ref.shape[1]
    rows = ncoord * LANES
    blk = min(SLOT_BLK, slots)

    def chunk(step, carry):
        start = pl.multiple_of(step * blk, blk)
        index = index_ref[:, pl.ds(start, blk)]
        high = index // LANES
        low = index % LANES
        onehot = (lax.broadcasted_iota(jnp.int32, (highs, blk), 0) == high).astype(jnp.bfloat16)
        match = lax.broadcasted_iota(jnp.int32, (LANES, blk), 0) == low
        grad = grad_ref[:, pl.ds(start, blk)]
        spread = jnp.concatenate(
            [jnp.where(match, grad[c:c + 1, :], 0.0) for c in range(ncoord)], axis=0
        )
        first, second, third = _split3(spread)
        weights = jnp.concatenate([first, second, third], axis=0)
        acc_ref[...] += lax.dot_general(
            weights, onehot, (((1,), (1,)), ((), ())), preferred_element_type=jnp.float32
        )
        return carry

    acc_ref[...] = jnp.zeros(acc_ref.shape, jnp.float32)
    lax.fori_loop(0, slots // blk, chunk, 0)
    acc = acc_ref[...]
    out_ref[...] = (acc[0:rows] + acc[rows:2 * rows]) + acc[2 * rows:3 * rows]


def scatter_points(grad, index, highs):
    ncoord, slots = grad.shape
    return pl.pallas_call(
        _scatter_kernel,
        out_shape=jax.ShapeDtypeStruct((ncoord * LANES, highs), jnp.float32),
        scratch_shapes=[pltpu.VMEM((3 * ncoord * LANES, highs), jnp.float32)],
    )(grad, index.reshape(1, slots))


@functools.partial(jax.custom_vjp, nondiff_argnums=(2,))
def take_points(table, index, highs):
    return gather_points(table, index)


def _take_fwd(table, index, highs):
    return gather_points(table, index), index


def _take_bwd(highs, index, grad):
    return scatter_points(grad, index, highs), None


take_points.defvjp(_take_fwd, _take_bwd)


def project(camera_tile, point_obs, observed):
    axis_angle = camera_tile[0:3]
    theta_sq = jnp.sum(axis_angle * axis_angle, axis=0)
    sine_term = (
        1.0
        - theta_sq / 6.0
        + theta_sq * theta_sq / 120.0
        - theta_sq * theta_sq * theta_sq / 5040.0
        + theta_sq * theta_sq * theta_sq * theta_sq / 362880.0
    )
    cosine_term = (
        0.5
        - theta_sq / 24.0
        + theta_sq * theta_sq / 720.0
        - theta_sq * theta_sq * theta_sq / 40320.0
        + theta_sq * theta_sq * theta_sq * theta_sq / 3628800.0
    )
    crossed = jnp.stack(
        [
            axis_angle[1] * point_obs[2] - axis_angle[2] * point_obs[1],
            axis_angle[2] * point_obs[0] - axis_angle[0] * point_obs[2],
            axis_angle[0] * point_obs[1] - axis_angle[1] * point_obs[0],
        ]
    )
    inner = jnp.sum(axis_angle * point_obs, axis=0)
    camera_frame = (
        point_obs
        + sine_term * crossed
        + cosine_term * (axis_angle * inner - theta_sq * point_obs)
        + camera_tile[3:6]
    )
    horizontal = camera_frame[0] / camera_frame[2]
    vertical = camera_frame[1] / camera_frame[2]
    radius_sq = horizontal * horizontal + vertical * vertical
    scale_term = camera_tile[6] * (
        1.0 + camera_tile[7] * radius_sq + camera_tile[8] * radius_sq * radius_sq
    )
    return jnp.stack([scale_term * horizontal - observed[0], scale_term * vertical - observed[1]])


def reweight(residual):
    return 1.0 / (1.0 + residual[0] * residual[0] + residual[1] * residual[1])


def adam_step(current, moment_one, moment_two, gradient):
    moment_one = 0.9 * moment_one + 0.1 * gradient
    moment_two = 0.999 * moment_two + 0.001 * gradient * gradient
    corrected_one = moment_one / (1.0 - 0.9**STEP)
    corrected_two = moment_two / (1.0 - 0.999**STEP)
    return (
        current - 0.05 * corrected_one / (jnp.sqrt(corrected_two) + 1e-08),
        moment_one,
        moment_two,
    )


def on_device(
    cameras,
    cam_first,
    cam_second,
    points,
    pt_first,
    pt_second,
    observed,
    tile_camera,
    point_index,
    tile_count,
):
    tile_num = tile_count.shape[0]
    tile_len = observed.shape[1] // tile_num
    obs_grid = observed.reshape(2, tile_num, tile_len)
    slot = lax.broadcasted_iota(jnp.int32, (tile_num, tile_len), 1)
    valid_mask = (slot < tile_count[:, None]).astype(jnp.float32)

    def residuals(camera_block, point_block):
        camera_tile = jnp.take(camera_block, tile_camera, axis=1)[:, :, None]
        point_obs = take_points(point_block, point_index, point_block.shape[1]).reshape(3, tile_num, tile_len)
        return project(camera_tile, point_obs, obs_grid)

    cam_rows, cam_cols = cameras.shape
    pt_rows, pt_cols = points.shape
    n_pt = lax.axis_size("pt")
    n_cam = lax.axis_size("cam")

    def doubling_gather(local, axis_name, size):
        me = lax.axis_index(axis_name)
        buf = local[None]
        dist = 1
        while dist < size:
            pairs = [(i, i ^ dist) for i in range(size)]
            other = lax.ppermute(buf, axis_name, pairs)
            low_half = (me // dist) % 2 == 0
            buf = jnp.where(
                low_half,
                jnp.concatenate([buf, other], axis=0),
                jnp.concatenate([other, buf], axis=0),
            )
            dist *= 2
        return buf

    def butterfly_sum(value, axis_name, size):
        dist = 1
        while dist < size:
            pairs = [(i, i ^ dist) for i in range(size)]
            value = value + lax.ppermute(value, axis_name, pairs)
            dist *= 2
        return value

    def gather_pts(local):
        rows = local.shape[0]
        flat = local.reshape(rows * pt_cols // LANES, LANES)
        stacked = doubling_gather(flat, "cam", n_cam)
        stacked = stacked.reshape(n_cam, rows, pt_cols // LANES, LANES)
        return stacked.transpose(1, 3, 0, 2).reshape(rows * LANES, n_cam * pt_cols // LANES)

    def own_pts(table):
        parts = table.reshape(pt_rows, LANES, n_cam, pt_cols // LANES)
        mine = lax.dynamic_index_in_dim(parts, lax.axis_index("cam"), axis=2, keepdims=False)
        return mine.transpose(0, 2, 1).reshape(pt_rows, pt_cols)

    def own_cams(block):
        start = lax.axis_index("pt") * cam_cols
        return lax.dynamic_slice_in_dim(block, start, cam_cols, axis=1)

    cam_state = jnp.concatenate([cameras, cam_first, cam_second], axis=0)
    cam_state = doubling_gather(cam_state, "pt", n_pt)
    cam_state = cam_state.transpose(1, 0, 2).reshape(3, cam_rows, n_pt * cam_cols)
    camera_block, first_block, second_block = cam_state[0], cam_state[1], cam_state[2]
    pt_state = gather_pts(jnp.concatenate([points, pt_first, pt_second], axis=0))
    pt_state = pt_state.reshape(3, pt_rows * LANES, pt_state.shape[1])
    point_block, pt_first_block, pt_second_block = pt_state[0], pt_state[1], pt_state[2]
    residual, pullback = jax.vjp(residuals, camera_block, point_block)
    cotangent = residual * (reweight(residual) * valid_mask)
    camera_grad, point_grad = pullback(cotangent)
    camera_grad = butterfly_sum(
        camera_grad.reshape(cam_rows * n_pt, cam_cols), "pt", n_pt
    ).reshape(cam_rows, n_pt * cam_cols)
    point_grad = butterfly_sum(point_grad, "cam", n_cam)
    new_cam_block, new_cam_first, new_cam_second = adam_step(
        camera_block, first_block, second_block, camera_grad
    )
    new_pt_block, new_pt_first, new_pt_second = adam_step(
        point_block, pt_first_block, pt_second_block, point_grad
    )
    new_cameras = own_cams(new_cam_block)
    new_cam_first = own_cams(new_cam_first)
    new_cam_second = own_cams(new_cam_second)
    new_points = own_pts(new_pt_block)
    new_pt_first = own_pts(new_pt_first)
    new_pt_second = own_pts(new_pt_second)
    final = residuals(new_cam_block, new_pt_block)
    final_weight = (reweight(final) * valid_mask).reshape(-1)
    final_residual = (final * valid_mask).reshape(2, -1)
    return (
        new_cameras,
        new_cam_first,
        new_cam_second,
        new_points,
        new_pt_first,
        new_pt_second,
        final_residual,
        final_weight,
    )


def solution(mesh):
    placed = (
        P(None, ("cam", "pt")),
        P(None, ("cam", "pt")),
        P(None, ("cam", "pt")),
        P(None, ("pt", "cam")),
        P(None, ("pt", "cam")),
        P(None, ("pt", "cam")),
        P(None, ("cam", "pt")),
        P(("cam", "pt")),
        P(("cam", "pt")),
        P(("cam", "pt")),
    )
    return jax.shard_map(
        on_device,
        mesh=mesh,
        in_specs=placed,
        out_specs=(
            P(None, ("cam", "pt")),
            P(None, ("cam", "pt")),
            P(None, ("cam", "pt")),
            P(None, ("pt", "cam")),
            P(None, ("pt", "cam")),
            P(None, ("pt", "cam")),
            P(None, ("cam", "pt")),
            P(("cam", "pt")),
        ),
        check_vma=False,
    )
```

```python
import functools

import jax
import jax.numpy as jnp
from jax import lax
from jax.sharding import PartitionSpec as P
from jax.experimental import pallas as pl
from jax.experimental.pallas import tpu as pltpu

STEP = 10
from jax.experimental import pallas as pl
from jax.experimental.pallas import tpu as pltpu

LANES = 128
SLOT_BLK = 1024


def _split3(x):
    first = x.astype(jnp.bfloat16)
    rest = x - first.astype(jnp.float32)
    second = rest.astype(jnp.bfloat16)
    third = (rest - second.astype(jnp.float32)).astype(jnp.bfloat16)
    return first, second, third


def _gather_kernel(table_ref, index_ref, out_ref, pieces_ref):
    rows = table_ref.shape[0]
    highs = table_ref.shape[1]

    @pl.when(pl.program_id(0) == 0)
    def _():
        first, second, third = _split3(table_ref[...])
        pieces_ref[0:rows, :] = first
        pieces_ref[rows:2 * rows, :] = second
        pieces_ref[2 * rows:3 * rows, :] = third

    index = index_ref[...]
    blk = index.shape[1]
    high = index // LANES
    low = index % LANES
    onehot = (lax.broadcasted_iota(jnp.int32, (highs, blk), 0) == high).astype(jnp.bfloat16)
    picked = jnp.dot(pieces_ref[...], onehot, preferred_element_type=jnp.float32)
    match = lax.broadcasted_iota(jnp.int32, (LANES, blk), 0) == low
    ncoord = rows // LANES
    sums = []
    for g in range(3 * ncoord):
        part = picked[g * LANES:(g + 1) * LANES, :]
        sums.append(jnp.sum(jnp.where(match, part, 0.0), axis=0, keepdims=True))
    for c in range(ncoord):
        out_ref[c:c + 1, :] = sums[c] + sums[ncoord + c] + sums[2 * ncoord + c]


def gather_points(table, index):
    ncoord = table.shape[0] // LANES
    highs = table.shape[1]
    slots = index.shape[0]
    blk = min(SLOT_BLK, slots)
    return pl.pallas_call(
        _gather_kernel,
        grid=(slots // blk,),
        in_specs=[
            pl.BlockSpec((ncoord * LANES, highs), lambda i: (0, 0)),
            pl.BlockSpec((1, blk), lambda i: (0, i)),
        ],
        out_specs=pl.BlockSpec((ncoord, blk), lambda i: (0, i)),
        out_shape=jax.ShapeDtypeStruct((ncoord, slots), jnp.float32),
        scratch_shapes=[pltpu.VMEM((3 * ncoord * LANES, highs), jnp.bfloat16)],
        compiler_params=pltpu.CompilerParams(dimension_semantics=("arbitrary",)),
    )(table, index.reshape(1, slots))


def _scatter_kernel(grad_ref, index_ref, out_ref, acc_ref):
    ncoord, slots = grad_ref.shape
    highs = out_ref.shape[1]
    rows = ncoord * LANES
    blk = min(SLOT_BLK, slots)

    def chunk(step, carry):
        start = pl.multiple_of(step * blk, blk)
        index = index_ref[:, pl.ds(start, blk)]
        high = index // LANES
        low = index % LANES
        onehot = (lax.broadcasted_iota(jnp.int32, (highs, blk), 0) == high).astype(jnp.bfloat16)
        match = lax.broadcasted_iota(jnp.int32, (LANES, blk), 0) == low
        grad = grad_ref[:, pl.ds(start, blk)]
        spread = jnp.concatenate(
            [jnp.where(match, grad[c:c + 1, :], 0.0) for c in range(ncoord)], axis=0
        )
        first, second, third = _split3(spread)
        weights = jnp.concatenate([first, second, third], axis=0)
        acc_ref[...] += lax.dot_general(
            weights, onehot, (((1,), (1,)), ((), ())), preferred_element_type=jnp.float32
        )
        return carry

    acc_ref[...] = jnp.zeros(acc_ref.shape, jnp.float32)
    lax.fori_loop(0, slots // blk, chunk, 0)
    acc = acc_ref[...]
    out_ref[...] = (acc[0:rows] + acc[rows:2 * rows]) + acc[2 * rows:3 * rows]


def scatter_points(grad, index, highs):
    ncoord, slots = grad.shape
    return pl.pallas_call(
        _scatter_kernel,
        out_shape=jax.ShapeDtypeStruct((ncoord * LANES, highs), jnp.float32),
        scratch_shapes=[pltpu.VMEM((3 * ncoord * LANES, highs), jnp.float32)],
    )(grad, index.reshape(1, slots))


@functools.partial(jax.custom_vjp, nondiff_argnums=(2,))
def take_points(table, index, highs):
    return gather_points(table, index)


def _take_fwd(table, index, highs):
    return gather_points(table, index), index


def _take_bwd(highs, index, grad):
    return scatter_points(grad, index, highs), None


take_points.defvjp(_take_fwd, _take_bwd)


def project(camera_tile, point_obs, observed):
    axis_angle = camera_tile[0:3]
    theta_sq = jnp.sum(axis_angle * axis_angle, axis=0)
    sine_term = (
        1.0
        - theta_sq / 6.0
        + theta_sq * theta_sq / 120.0
        - theta_sq * theta_sq * theta_sq / 5040.0
        + theta_sq * theta_sq * theta_sq * theta_sq / 362880.0
    )
    cosine_term = (
        0.5
        - theta_sq / 24.0
        + theta_sq * theta_sq / 720.0
        - theta_sq * theta_sq * theta_sq / 40320.0
        + theta_sq * theta_sq * theta_sq * theta_sq / 3628800.0
    )
    crossed = jnp.stack(
        [
            axis_angle[1] * point_obs[2] - axis_angle[2] * point_obs[1],
            axis_angle[2] * point_obs[0] - axis_angle[0] * point_obs[2],
            axis_angle[0] * point_obs[1] - axis_angle[1] * point_obs[0],
        ]
    )
    inner = jnp.sum(axis_angle * point_obs, axis=0)
    camera_frame = (
        point_obs
        + sine_term * crossed
        + cosine_term * (axis_angle * inner - theta_sq * point_obs)
        + camera_tile[3:6]
    )
    horizontal = camera_frame[0] / camera_frame[2]
    vertical = camera_frame[1] / camera_frame[2]
    radius_sq = horizontal * horizontal + vertical * vertical
    scale_term = camera_tile[6] * (
        1.0 + camera_tile[7] * radius_sq + camera_tile[8] * radius_sq * radius_sq
    )
    return jnp.stack([scale_term * horizontal - observed[0], scale_term * vertical - observed[1]])


def reweight(residual):
    return 1.0 / (1.0 + residual[0] * residual[0] + residual[1] * residual[1])


def adam_step(current, moment_one, moment_two, gradient):
    moment_one = 0.9 * moment_one + 0.1 * gradient
    moment_two = 0.999 * moment_two + 0.001 * gradient * gradient
    corrected_one = moment_one / (1.0 - 0.9**STEP)
    corrected_two = moment_two / (1.0 - 0.999**STEP)
    return (
        current - 0.05 * corrected_one / (jnp.sqrt(corrected_two) + 1e-08),
        moment_one,
        moment_two,
    )


def on_device(
    cameras,
    cam_first,
    cam_second,
    points,
    pt_first,
    pt_second,
    observed,
    tile_camera,
    point_index,
    tile_count,
):
    tile_num = tile_count.shape[0]
    tile_len = observed.shape[1] // tile_num
    obs_grid = observed.reshape(2, tile_num, tile_len)
    slot = lax.broadcasted_iota(jnp.int32, (tile_num, tile_len), 1)
    valid_mask = (slot < tile_count[:, None]).astype(jnp.float32)

    def residuals(camera_block, point_block):
        camera_tile = jnp.take(camera_block, tile_camera, axis=1)[:, :, None]
        point_obs = take_points(point_block, point_index, point_block.shape[1]).reshape(3, tile_num, tile_len)
        return project(camera_tile, point_obs, obs_grid)

    cam_rows, cam_cols = cameras.shape
    pt_rows, pt_cols = points.shape
    n_pt = lax.axis_size("pt")
    n_cam = lax.axis_size("cam")

    def doubling_gather(local, axis_name, size):
        me = lax.axis_index(axis_name)
        buf = local[None]
        dist = 1
        while dist < size:
            pairs = [(i, i ^ dist) for i in range(size)]
            other = lax.ppermute(buf, axis_name, pairs)
            low_half = (me // dist) % 2 == 0
            buf = jnp.where(
                low_half,
                jnp.concatenate([buf, other], axis=0),
                jnp.concatenate([other, buf], axis=0),
            )
            dist *= 2
        return buf

    def butterfly_sum(value, axis_name, size):
        dist = 1
        while dist < size:
            pairs = [(i, i ^ dist) for i in range(size)]
            value = value + lax.ppermute(value, axis_name, pairs)
            dist *= 2
        return value

    def gather_pts(local):
        flat = local.reshape(pt_rows * pt_cols // LANES, LANES)
        stacked = doubling_gather(flat, "cam", n_cam)
        stacked = stacked.reshape(n_cam, pt_rows, pt_cols // LANES, LANES)
        return stacked.transpose(1, 3, 0, 2).reshape(pt_rows * LANES, n_cam * pt_cols // LANES)

    def own_pts(table):
        parts = table.reshape(pt_rows, LANES, n_cam, pt_cols // LANES)
        mine = lax.dynamic_index_in_dim(parts, lax.axis_index("cam"), axis=2, keepdims=False)
        return mine.transpose(0, 2, 1).reshape(pt_rows, pt_cols)

    def own_cams(block):
        start = lax.axis_index("pt") * cam_cols
        return lax.dynamic_slice_in_dim(block, start, cam_cols, axis=1)

    cam_state = jnp.concatenate([cameras, cam_first, cam_second], axis=0)
    cam_state = doubling_gather(cam_state, "pt", n_pt)
    cam_state = cam_state.transpose(1, 0, 2).reshape(3, cam_rows, n_pt * cam_cols)
    camera_block, first_block, second_block = cam_state[0], cam_state[1], cam_state[2]
    point_block = gather_pts(points)
    residual, pullback = jax.vjp(residuals, camera_block, point_block)
    cotangent = residual * (reweight(residual) * valid_mask)
    camera_grad, point_grad = lax.optimization_barrier(pullback(cotangent))
    camera_grad = butterfly_sum(
        camera_grad.reshape(cam_rows * n_pt, cam_cols), "pt", n_pt
    ).reshape(cam_rows, n_pt * cam_cols)
    point_grad = butterfly_sum(point_grad, "cam", n_cam)
    new_cam_block, new_cam_first, new_cam_second = adam_step(
        camera_block, first_block, second_block, camera_grad
    )
    new_pt_block, new_pt_first, new_pt_second = adam_step(
        point_block, gather_pts(pt_first), gather_pts(pt_second), point_grad
    )
    new_cameras = own_cams(new_cam_block)
    new_cam_first = own_cams(new_cam_first)
    new_cam_second = own_cams(new_cam_second)
    new_points = own_pts(new_pt_block)
    new_pt_first = own_pts(new_pt_first)
    new_pt_second = own_pts(new_pt_second)
    final = residuals(new_cam_block, new_pt_block)
    final_weight = (reweight(final) * valid_mask).reshape(-1)
    final_residual = (final * valid_mask).reshape(2, -1)
    return (
        new_cameras,
        new_cam_first,
        new_cam_second,
        new_points,
        new_pt_first,
        new_pt_second,
        final_residual,
        final_weight,
    )


def solution(mesh):
    placed = (
        P(None, ("cam", "pt")),
        P(None, ("cam", "pt")),
        P(None, ("cam", "pt")),
        P(None, ("pt", "cam")),
        P(None, ("pt", "cam")),
        P(None, ("pt", "cam")),
        P(None, ("cam", "pt")),
        P(("cam", "pt")),
        P(("cam", "pt")),
        P(("cam", "pt")),
    )
    return jax.shard_map(
        on_device,
        mesh=mesh,
        in_specs=placed,
        out_specs=(
            P(None, ("cam", "pt")),
            P(None, ("cam", "pt")),
            P(None, ("cam", "pt")),
            P(None, ("pt", "cam")),
            P(None, ("pt", "cam")),
            P(None, ("pt", "cam")),
            P(None, ("cam", "pt")),
            P(("cam", "pt")),
        ),
        check_vma=False,
    )
```

```python
import functools

import jax
import jax.numpy as jnp
from jax import lax
from jax.sharding import PartitionSpec as P
from jax.experimental import pallas as pl
from jax.experimental.pallas import tpu as pltpu

STEP = 10
from jax.experimental import pallas as pl
from jax.experimental.pallas import tpu as pltpu

LANES = 128
SLOT_BLK = 1024


def _split3(x):
    first = x.astype(jnp.bfloat16)
    rest = x - first.astype(jnp.float32)
    second = rest.astype(jnp.bfloat16)
    third = (rest - second.astype(jnp.float32)).astype(jnp.bfloat16)
    return first, second, third


def _gather_kernel(table_ref, index_ref, out_ref, pieces_ref):
    rows = table_ref.shape[0]
    highs = table_ref.shape[1]

    @pl.when(pl.program_id(0) == 0)
    def _():
        first, second, third = _split3(table_ref[...])
        pieces_ref[0:rows, :] = first
        pieces_ref[rows:2 * rows, :] = second
        pieces_ref[2 * rows:3 * rows, :] = third

    index = index_ref[...]
    blk = index.shape[1]
    high = index // LANES
    low = index % LANES
    onehot = (lax.broadcasted_iota(jnp.int32, (highs, blk), 0) == high).astype(jnp.bfloat16)
    picked = jnp.dot(pieces_ref[...], onehot, preferred_element_type=jnp.float32)
    match = lax.broadcasted_iota(jnp.int32, (LANES, blk), 0) == low
    ncoord = rows // LANES
    sums = []
    for g in range(3 * ncoord):
        part = picked[g * LANES:(g + 1) * LANES, :]
        sums.append(jnp.sum(jnp.where(match, part, 0.0), axis=0, keepdims=True))
    for c in range(ncoord):
        out_ref[c:c + 1, :] = sums[c] + sums[ncoord + c] + sums[2 * ncoord + c]


def gather_points(table, index):
    ncoord = table.shape[0] // LANES
    highs = table.shape[1]
    slots = index.shape[0]
    blk = min(SLOT_BLK, slots)
    return pl.pallas_call(
        _gather_kernel,
        grid=(slots // blk,),
        in_specs=[
            pl.BlockSpec((ncoord * LANES, highs), lambda i: (0, 0)),
            pl.BlockSpec((1, blk), lambda i: (0, i)),
        ],
        out_specs=pl.BlockSpec((ncoord, blk), lambda i: (0, i)),
        out_shape=jax.ShapeDtypeStruct((ncoord, slots), jnp.float32),
        scratch_shapes=[pltpu.VMEM((3 * ncoord * LANES, highs), jnp.bfloat16)],
        compiler_params=pltpu.CompilerParams(dimension_semantics=("arbitrary",)),
    )(table, index.reshape(1, slots))


def _scatter_kernel(grad_ref, index_ref, out_ref, acc_ref):
    ncoord, slots = grad_ref.shape
    highs = out_ref.shape[1]
    rows = ncoord * LANES
    blk = min(SLOT_BLK, slots)

    def chunk(step, carry):
        start = pl.multiple_of(step * blk, blk)
        index = index_ref[:, pl.ds(start, blk)]
        high = index // LANES
        low = index % LANES
        onehot = (lax.broadcasted_iota(jnp.int32, (highs, blk), 0) == high).astype(jnp.bfloat16)
        match = lax.broadcasted_iota(jnp.int32, (LANES, blk), 0) == low
        grad = grad_ref[:, pl.ds(start, blk)]
        spread = jnp.concatenate(
            [jnp.where(match, grad[c:c + 1, :], 0.0) for c in range(ncoord)], axis=0
        )
        first, second, third = _split3(spread)
        weights = jnp.concatenate([first, second, third], axis=0)
        acc_ref[...] += lax.dot_general(
            weights, onehot, (((1,), (1,)), ((), ())), preferred_element_type=jnp.float32
        )
        return carry

    acc_ref[...] = jnp.zeros(acc_ref.shape, jnp.float32)
    lax.fori_loop(0, slots // blk, chunk, 0)
    acc = acc_ref[...]
    out_ref[...] = (acc[0:rows] + acc[rows:2 * rows]) + acc[2 * rows:3 * rows]


def scatter_points(grad, index, highs):
    ncoord, slots = grad.shape
    return pl.pallas_call(
        _scatter_kernel,
        out_shape=jax.ShapeDtypeStruct((ncoord * LANES, highs), jnp.float32),
        scratch_shapes=[pltpu.VMEM((3 * ncoord * LANES, highs), jnp.float32)],
    )(grad, index.reshape(1, slots))


@functools.partial(jax.custom_vjp, nondiff_argnums=(2,))
def take_points(table, index, highs):
    return gather_points(table, index)


def _take_fwd(table, index, highs):
    return gather_points(table, index), index


def _take_bwd(highs, index, grad):
    return scatter_points(grad, index, highs), None


take_points.defvjp(_take_fwd, _take_bwd)


def project(camera_tile, point_obs, observed):
    axis_angle = camera_tile[0:3]
    theta_sq = jnp.sum(axis_angle * axis_angle, axis=0)
    sine_term = (
        1.0
        - theta_sq / 6.0
        + theta_sq * theta_sq / 120.0
        - theta_sq * theta_sq * theta_sq / 5040.0
        + theta_sq * theta_sq * theta_sq * theta_sq / 362880.0
    )
    cosine_term = (
        0.5
        - theta_sq / 24.0
        + theta_sq * theta_sq / 720.0
        - theta_sq * theta_sq * theta_sq / 40320.0
        + theta_sq * theta_sq * theta_sq * theta_sq / 3628800.0
    )
    crossed = jnp.stack(
        [
            axis_angle[1] * point_obs[2] - axis_angle[2] * point_obs[1],
            axis_angle[2] * point_obs[0] - axis_angle[0] * point_obs[2],
            axis_angle[0] * point_obs[1] - axis_angle[1] * point_obs[0],
        ]
    )
    inner = jnp.sum(axis_angle * point_obs, axis=0)
    camera_frame = (
        point_obs
        + sine_term * crossed
        + cosine_term * (axis_angle * inner - theta_sq * point_obs)
        + camera_tile[3:6]
    )
    horizontal = camera_frame[0] / camera_frame[2]
    vertical = camera_frame[1] / camera_frame[2]
    radius_sq = horizontal * horizontal + vertical * vertical
    scale_term = camera_tile[6] * (
        1.0 + camera_tile[7] * radius_sq + camera_tile[8] * radius_sq * radius_sq
    )
    return jnp.stack([scale_term * horizontal - observed[0], scale_term * vertical - observed[1]])


def reweight(residual):
    return 1.0 / (1.0 + residual[0] * residual[0] + residual[1] * residual[1])


def adam_step(current, moment_one, moment_two, gradient):
    moment_one = 0.9 * moment_one + 0.1 * gradient
    moment_two = 0.999 * moment_two + 0.001 * gradient * gradient
    corrected_one = moment_one / (1.0 - 0.9**STEP)
    corrected_two = moment_two / (1.0 - 0.999**STEP)
    return (
        current - 0.05 * corrected_one / (jnp.sqrt(corrected_two) + 1e-08),
        moment_one,
        moment_two,
    )


def on_device(
    cameras,
    cam_first,
    cam_second,
    points,
    pt_first,
    pt_second,
    observed,
    tile_camera,
    point_index,
    tile_count,
):
    tile_num = tile_count.shape[0]
    tile_len = observed.shape[1] // tile_num
    obs_grid = observed.reshape(2, tile_num, tile_len)
    slot = lax.broadcasted_iota(jnp.int32, (tile_num, tile_len), 1)
    valid_mask = (slot < tile_count[:, None]).astype(jnp.float32)

    def residuals(camera_block, point_block):
        camera_tile = jnp.take(camera_block, tile_camera, axis=1)[:, :, None]
        point_obs = take_points(point_block, point_index, point_block.shape[1]).reshape(3, tile_num, tile_len)
        return project(camera_tile, point_obs, obs_grid)

    cam_rows, cam_cols = cameras.shape
    pt_rows, pt_cols = points.shape
    n_pt = lax.axis_size("pt")
    n_cam = lax.axis_size("cam")

    def doubling_gather(local, axis_name, size):
        me = lax.axis_index(axis_name)
        buf = local[None]
        dist = 1
        while dist < size:
            pairs = [(i, i ^ dist) for i in range(size)]
            other = lax.ppermute(buf, axis_name, pairs)
            low_half = (me // dist) % 2 == 0
            buf = jnp.where(
                low_half,
                jnp.concatenate([buf, other], axis=0),
                jnp.concatenate([other, buf], axis=0),
            )
            dist *= 2
        return buf

    def butterfly_sum(value, axis_name, size):
        dist = 1
        while dist < size:
            pairs = [(i, i ^ dist) for i in range(size)]
            value = value + lax.ppermute(value, axis_name, pairs)
            dist *= 2
        return value

    def gather_pts(local):
        rows = local.shape[0]
        flat = local.reshape(rows * pt_cols // LANES, LANES)
        stacked = doubling_gather(flat, "cam", n_cam)
        stacked = stacked.reshape(n_cam, rows, pt_cols // LANES, LANES)
        return stacked.transpose(1, 3, 0, 2).reshape(rows * LANES, n_cam * pt_cols // LANES)

    def own_pts(table):
        parts = table.reshape(pt_rows, LANES, n_cam, pt_cols // LANES)
        mine = lax.dynamic_index_in_dim(parts, lax.axis_index("cam"), axis=2, keepdims=False)
        return mine.transpose(0, 2, 1).reshape(pt_rows, pt_cols)

    def own_cams(block):
        start = lax.axis_index("pt") * cam_cols
        return lax.dynamic_slice_in_dim(block, start, cam_cols, axis=1)

    cam_state = jnp.concatenate([cameras, cam_first, cam_second], axis=0)
    cam_state = doubling_gather(cam_state, "pt", n_pt)
    cam_state = cam_state.transpose(1, 0, 2).reshape(3, cam_rows, n_pt * cam_cols)
    camera_block, first_block, second_block = cam_state[0], cam_state[1], cam_state[2]
    point_block = gather_pts(points)
    residual, pullback = jax.vjp(residuals, camera_block, point_block)
    cotangent = residual * (reweight(residual) * valid_mask)
    camera_grad, point_grad = pullback(cotangent)
    camera_grad = butterfly_sum(
        camera_grad.reshape(cam_rows * n_pt, cam_cols), "pt", n_pt
    ).reshape(cam_rows, n_pt * cam_cols)
    point_grad = butterfly_sum(point_grad, "cam", n_cam)
    new_cam_block, new_cam_first, new_cam_second = adam_step(
        camera_block, first_block, second_block, camera_grad
    )
    moments = gather_pts(jnp.concatenate([pt_first, pt_second], axis=0))
    moments = moments.reshape(2, pt_rows * LANES, moments.shape[1])
    new_pt_block, new_pt_first, new_pt_second = adam_step(
        point_block, moments[0], moments[1], point_grad
    )
    new_cameras = own_cams(new_cam_block)
    new_cam_first = own_cams(new_cam_first)
    new_cam_second = own_cams(new_cam_second)
    new_points = own_pts(new_pt_block)
    new_pt_first = own_pts(new_pt_first)
    new_pt_second = own_pts(new_pt_second)
    final = residuals(new_cam_block, new_pt_block)
    final_weight = (reweight(final) * valid_mask).reshape(-1)
    final_residual = (final * valid_mask).reshape(2, -1)
    return (
        new_cameras,
        new_cam_first,
        new_cam_second,
        new_points,
        new_pt_first,
        new_pt_second,
        final_residual,
        final_weight,
    )


def solution(mesh):
    placed = (
        P(None, ("cam", "pt")),
        P(None, ("cam", "pt")),
        P(None, ("cam", "pt")),
        P(None, ("pt", "cam")),
        P(None, ("pt", "cam")),
        P(None, ("pt", "cam")),
        P(None, ("cam", "pt")),
        P(("cam", "pt")),
        P(("cam", "pt")),
        P(("cam", "pt")),
    )
    return jax.shard_map(
        on_device,
        mesh=mesh,
        in_specs=placed,
        out_specs=(
            P(None, ("cam", "pt")),
            P(None, ("cam", "pt")),
            P(None, ("cam", "pt")),
            P(None, ("pt", "cam")),
            P(None, ("pt", "cam")),
            P(None, ("pt", "cam")),
            P(None, ("cam", "pt")),
            P(("cam", "pt")),
        ),
        check_vma=False,
    )
```

```python
import functools

import jax
import jax.numpy as jnp
from jax import lax
from jax.sharding import PartitionSpec as P
from jax.experimental import pallas as pl
from jax.experimental.pallas import tpu as pltpu

STEP = 10
from jax.experimental import pallas as pl
from jax.experimental.pallas import tpu as pltpu

LANES = 128
SLOT_BLK = 2048


def _split3(x):
    first = x.astype(jnp.bfloat16)
    rest = x - first.astype(jnp.float32)
    second = rest.astype(jnp.bfloat16)
    third = (rest - second.astype(jnp.float32)).astype(jnp.bfloat16)
    return first, second, third


def _gather_kernel(table_ref, index_ref, out_ref, pieces_ref):
    rows = table_ref.shape[0]
    highs = table_ref.shape[1]

    @pl.when(pl.program_id(0) == 0)
    def _():
        first, second, third = _split3(table_ref[...])
        pieces_ref[0:rows, :] = first
        pieces_ref[rows:2 * rows, :] = second
        pieces_ref[2 * rows:3 * rows, :] = third

    index = index_ref[...]
    blk = index.shape[1]
    high = index // LANES
    low = index % LANES
    onehot = (lax.broadcasted_iota(jnp.int32, (highs, blk), 0) == high).astype(jnp.bfloat16)
    picked = jnp.dot(pieces_ref[...], onehot, preferred_element_type=jnp.float32)
    match = lax.broadcasted_iota(jnp.int32, (LANES, blk), 0) == low
    ncoord = rows // LANES
    sums = []
    for g in range(3 * ncoord):
        part = picked[g * LANES:(g + 1) * LANES, :]
        sums.append(jnp.sum(jnp.where(match, part, 0.0), axis=0, keepdims=True))
    for c in range(ncoord):
        out_ref[c:c + 1, :] = sums[c] + sums[ncoord + c] + sums[2 * ncoord + c]


def gather_points(table, index):
    ncoord = table.shape[0] // LANES
    highs = table.shape[1]
    slots = index.shape[0]
    blk = min(SLOT_BLK, slots)
    return pl.pallas_call(
        _gather_kernel,
        grid=(slots // blk,),
        in_specs=[
            pl.BlockSpec((ncoord * LANES, highs), lambda i: (0, 0)),
            pl.BlockSpec((1, blk), lambda i: (0, i)),
        ],
        out_specs=pl.BlockSpec((ncoord, blk), lambda i: (0, i)),
        out_shape=jax.ShapeDtypeStruct((ncoord, slots), jnp.float32),
        scratch_shapes=[pltpu.VMEM((3 * ncoord * LANES, highs), jnp.bfloat16)],
        compiler_params=pltpu.CompilerParams(dimension_semantics=("arbitrary",)),
    )(table, index.reshape(1, slots))


def _scatter_kernel(grad_ref, index_ref, out_ref, acc_ref):
    ncoord, slots = grad_ref.shape
    highs = out_ref.shape[1]
    rows = ncoord * LANES
    blk = min(SLOT_BLK, slots)

    def chunk(step, carry):
        start = pl.multiple_of(step * blk, blk)
        index = index_ref[:, pl.ds(start, blk)]
        high = index // LANES
        low = index % LANES
        onehot = (lax.broadcasted_iota(jnp.int32, (highs, blk), 0) == high).astype(jnp.bfloat16)
        match = lax.broadcasted_iota(jnp.int32, (LANES, blk), 0) == low
        grad = grad_ref[:, pl.ds(start, blk)]
        spread = jnp.concatenate(
            [jnp.where(match, grad[c:c + 1, :], 0.0) for c in range(ncoord)], axis=0
        )
        first, second, third = _split3(spread)
        weights = jnp.concatenate([first, second, third], axis=0)
        acc_ref[...] += lax.dot_general(
            weights, onehot, (((1,), (1,)), ((), ())), preferred_element_type=jnp.float32
        )
        return carry

    acc_ref[...] = jnp.zeros(acc_ref.shape, jnp.float32)
    lax.fori_loop(0, slots // blk, chunk, 0)
    acc = acc_ref[...]
    out_ref[...] = (acc[0:rows] + acc[rows:2 * rows]) + acc[2 * rows:3 * rows]


def scatter_points(grad, index, highs):
    ncoord, slots = grad.shape
    return pl.pallas_call(
        _scatter_kernel,
        out_shape=jax.ShapeDtypeStruct((ncoord * LANES, highs), jnp.float32),
        scratch_shapes=[pltpu.VMEM((3 * ncoord * LANES, highs), jnp.float32)],
    )(grad, index.reshape(1, slots))


@functools.partial(jax.custom_vjp, nondiff_argnums=(2,))
def take_points(table, index, highs):
    return gather_points(table, index)


def _take_fwd(table, index, highs):
    return gather_points(table, index), index


def _take_bwd(highs, index, grad):
    return scatter_points(grad, index, highs), None


take_points.defvjp(_take_fwd, _take_bwd)


def project(camera_tile, point_obs, observed):
    axis_angle = camera_tile[0:3]
    theta_sq = jnp.sum(axis_angle * axis_angle, axis=0)
    sine_term = (
        1.0
        - theta_sq / 6.0
        + theta_sq * theta_sq / 120.0
        - theta_sq * theta_sq * theta_sq / 5040.0
        + theta_sq * theta_sq * theta_sq * theta_sq / 362880.0
    )
    cosine_term = (
        0.5
        - theta_sq / 24.0
        + theta_sq * theta_sq / 720.0
        - theta_sq * theta_sq * theta_sq / 40320.0
        + theta_sq * theta_sq * theta_sq * theta_sq / 3628800.0
    )
    crossed = jnp.stack(
        [
            axis_angle[1] * point_obs[2] - axis_angle[2] * point_obs[1],
            axis_angle[2] * point_obs[0] - axis_angle[0] * point_obs[2],
            axis_angle[0] * point_obs[1] - axis_angle[1] * point_obs[0],
        ]
    )
    inner = jnp.sum(axis_angle * point_obs, axis=0)
    camera_frame = (
        point_obs
        + sine_term * crossed
        + cosine_term * (axis_angle * inner - theta_sq * point_obs)
        + camera_tile[3:6]
    )
    horizontal = camera_frame[0] / camera_frame[2]
    vertical = camera_frame[1] / camera_frame[2]
    radius_sq = horizontal * horizontal + vertical * vertical
    scale_term = camera_tile[6] * (
        1.0 + camera_tile[7] * radius_sq + camera_tile[8] * radius_sq * radius_sq
    )
    return jnp.stack([scale_term * horizontal - observed[0], scale_term * vertical - observed[1]])


def reweight(residual):
    return 1.0 / (1.0 + residual[0] * residual[0] + residual[1] * residual[1])


def adam_step(current, moment_one, moment_two, gradient):
    moment_one = 0.9 * moment_one + 0.1 * gradient
    moment_two = 0.999 * moment_two + 0.001 * gradient * gradient
    corrected_one = moment_one / (1.0 - 0.9**STEP)
    corrected_two = moment_two / (1.0 - 0.999**STEP)
    return (
        current - 0.05 * corrected_one / (jnp.sqrt(corrected_two) + 1e-08),
        moment_one,
        moment_two,
    )


def on_device(
    cameras,
    cam_first,
    cam_second,
    points,
    pt_first,
    pt_second,
    observed,
    tile_camera,
    point_index,
    tile_count,
):
    tile_num = tile_count.shape[0]
    tile_len = observed.shape[1] // tile_num
    obs_grid = observed.reshape(2, tile_num, tile_len)
    slot = lax.broadcasted_iota(jnp.int32, (tile_num, tile_len), 1)
    valid_mask = (slot < tile_count[:, None]).astype(jnp.float32)

    def residuals(camera_block, point_block):
        camera_tile = jnp.take(camera_block, tile_camera, axis=1)[:, :, None]
        point_obs = take_points(point_block, point_index, point_block.shape[1]).reshape(3, tile_num, tile_len)
        return project(camera_tile, point_obs, obs_grid)

    cam_rows, cam_cols = cameras.shape
    pt_rows, pt_cols = points.shape
    n_pt = lax.axis_size("pt")
    n_cam = lax.axis_size("cam")

    def doubling_gather(local, axis_name, size):
        me = lax.axis_index(axis_name)
        buf = local[None]
        dist = 1
        while dist < size:
            pairs = [(i, i ^ dist) for i in range(size)]
            other = lax.ppermute(buf, axis_name, pairs)
            low_half = (me // dist) % 2 == 0
            buf = jnp.where(
                low_half,
                jnp.concatenate([buf, other], axis=0),
                jnp.concatenate([other, buf], axis=0),
            )
            dist *= 2
        return buf

    def butterfly_sum(value, axis_name, size):
        dist = 1
        while dist < size:
            pairs = [(i, i ^ dist) for i in range(size)]
            value = value + lax.ppermute(value, axis_name, pairs)
            dist *= 2
        return value

    def gather_pts(local):
        rows = local.shape[0]
        flat = local.reshape(rows * pt_cols // LANES, LANES)
        stacked = doubling_gather(flat, "cam", n_cam)
        stacked = stacked.reshape(n_cam, rows, pt_cols // LANES, LANES)
        return stacked.transpose(1, 3, 0, 2).reshape(rows * LANES, n_cam * pt_cols // LANES)

    def own_pts(table):
        parts = table.reshape(pt_rows, LANES, n_cam, pt_cols // LANES)
        mine = lax.dynamic_index_in_dim(parts, lax.axis_index("cam"), axis=2, keepdims=False)
        return mine.transpose(0, 2, 1).reshape(pt_rows, pt_cols)

    def own_cams(block):
        start = lax.axis_index("pt") * cam_cols
        return lax.dynamic_slice_in_dim(block, start, cam_cols, axis=1)

    cam_state = jnp.concatenate([cameras, cam_first, cam_second], axis=0)
    cam_state = doubling_gather(cam_state, "pt", n_pt)
    cam_state = cam_state.transpose(1, 0, 2).reshape(3, cam_rows, n_pt * cam_cols)
    camera_block, first_block, second_block = cam_state[0], cam_state[1], cam_state[2]
    point_block = gather_pts(points)
    residual, pullback = jax.vjp(residuals, camera_block, point_block)
    cotangent = residual * (reweight(residual) * valid_mask)
    camera_grad, point_grad = pullback(cotangent)
    camera_grad = butterfly_sum(
        camera_grad.reshape(cam_rows * n_pt, cam_cols), "pt", n_pt
    ).reshape(cam_rows, n_pt * cam_cols)
    point_grad = butterfly_sum(point_grad, "cam", n_cam)
    new_cam_block, new_cam_first, new_cam_second = adam_step(
        camera_block, first_block, second_block, camera_grad
    )
    moments = gather_pts(jnp.concatenate([pt_first, pt_second], axis=0))
    moments = moments.reshape(2, pt_rows * LANES, moments.shape[1])
    new_pt_block, new_pt_first, new_pt_second = adam_step(
        point_block, moments[0], moments[1], point_grad
    )
    new_cameras = own_cams(new_cam_block)
    new_cam_first = own_cams(new_cam_first)
    new_cam_second = own_cams(new_cam_second)
    new_points = own_pts(new_pt_block)
    new_pt_first = own_pts(new_pt_first)
    new_pt_second = own_pts(new_pt_second)
    final = residuals(new_cam_block, new_pt_block)
    final_weight = (reweight(final) * valid_mask).reshape(-1)
    final_residual = (final * valid_mask).reshape(2, -1)
    return (
        new_cameras,
        new_cam_first,
        new_cam_second,
        new_points,
        new_pt_first,
        new_pt_second,
        final_residual,
        final_weight,
    )


def solution(mesh):
    placed = (
        P(None, ("cam", "pt")),
        P(None, ("cam", "pt")),
        P(None, ("cam", "pt")),
        P(None, ("pt", "cam")),
        P(None, ("pt", "cam")),
        P(None, ("pt", "cam")),
        P(None, ("cam", "pt")),
        P(("cam", "pt")),
        P(("cam", "pt")),
        P(("cam", "pt")),
    )
    return jax.shard_map(
        on_device,
        mesh=mesh,
        in_specs=placed,
        out_specs=(
            P(None, ("cam", "pt")),
            P(None, ("cam", "pt")),
            P(None, ("cam", "pt")),
            P(None, ("pt", "cam")),
            P(None, ("pt", "cam")),
            P(None, ("pt", "cam")),
            P(None, ("cam", "pt")),
            P(("cam", "pt")),
        ),
        check_vma=False,
    )
```

```python
import functools

import jax
import jax.numpy as jnp
from jax import lax
from jax.sharding import PartitionSpec as P
from jax.experimental import pallas as pl
from jax.experimental.pallas import tpu as pltpu

STEP = 10
from jax.experimental import pallas as pl
from jax.experimental.pallas import tpu as pltpu

LANES = 128
SLOT_BLK = 4096


def _split3(x):
    first = x.astype(jnp.bfloat16)
    rest = x - first.astype(jnp.float32)
    second = rest.astype(jnp.bfloat16)
    third = (rest - second.astype(jnp.float32)).astype(jnp.bfloat16)
    return first, second, third


def _gather_kernel(table_ref, index_ref, out_ref, pieces_ref):
    rows = table_ref.shape[0]
    highs = table_ref.shape[1]

    @pl.when(pl.program_id(0) == 0)
    def _():
        first, second, third = _split3(table_ref[...])
        pieces_ref[0:rows, :] = first
        pieces_ref[rows:2 * rows, :] = second
        pieces_ref[2 * rows:3 * rows, :] = third

    index = index_ref[...]
    blk = index.shape[1]
    high = index // LANES
    low = index % LANES
    onehot = (lax.broadcasted_iota(jnp.int32, (highs, blk), 0) == high).astype(jnp.bfloat16)
    picked = jnp.dot(pieces_ref[...], onehot, preferred_element_type=jnp.float32)
    match = lax.broadcasted_iota(jnp.int32, (LANES, blk), 0) == low
    ncoord = rows // LANES
    sums = []
    for g in range(3 * ncoord):
        part = picked[g * LANES:(g + 1) * LANES, :]
        sums.append(jnp.sum(jnp.where(match, part, 0.0), axis=0, keepdims=True))
    for c in range(ncoord):
        out_ref[c:c + 1, :] = sums[c] + sums[ncoord + c] + sums[2 * ncoord + c]


def gather_points(table, index):
    ncoord = table.shape[0] // LANES
    highs = table.shape[1]
    slots = index.shape[0]
    blk = min(SLOT_BLK, slots)
    return pl.pallas_call(
        _gather_kernel,
        grid=(slots // blk,),
        in_specs=[
            pl.BlockSpec((ncoord * LANES, highs), lambda i: (0, 0)),
            pl.BlockSpec((1, blk), lambda i: (0, i)),
        ],
        out_specs=pl.BlockSpec((ncoord, blk), lambda i: (0, i)),
        out_shape=jax.ShapeDtypeStruct((ncoord, slots), jnp.float32),
        scratch_shapes=[pltpu.VMEM((3 * ncoord * LANES, highs), jnp.bfloat16)],
        compiler_params=pltpu.CompilerParams(dimension_semantics=("arbitrary",)),
    )(table, index.reshape(1, slots))


def _scatter_kernel(grad_ref, index_ref, out_ref, acc_ref):
    ncoord, slots = grad_ref.shape
    highs = out_ref.shape[1]
    rows = ncoord * LANES
    blk = min(SLOT_BLK, slots)

    def chunk(step, carry):
        start = pl.multiple_of(step * blk, blk)
        index = index_ref[:, pl.ds(start, blk)]
        high = index // LANES
        low = index % LANES
        onehot = (lax.broadcasted_iota(jnp.int32, (highs, blk), 0) == high).astype(jnp.bfloat16)
        match = lax.broadcasted_iota(jnp.int32, (LANES, blk), 0) == low
        grad = grad_ref[:, pl.ds(start, blk)]
        spread = jnp.concatenate(
            [jnp.where(match, grad[c:c + 1, :], 0.0) for c in range(ncoord)], axis=0
        )
        first, second, third = _split3(spread)
        weights = jnp.concatenate([first, second, third], axis=0)
        acc_ref[...] += lax.dot_general(
            weights, onehot, (((1,), (1,)), ((), ())), preferred_element_type=jnp.float32
        )
        return carry

    acc_ref[...] = jnp.zeros(acc_ref.shape, jnp.float32)
    lax.fori_loop(0, slots // blk, chunk, 0)
    acc = acc_ref[...]
    out_ref[...] = (acc[0:rows] + acc[rows:2 * rows]) + acc[2 * rows:3 * rows]


def scatter_points(grad, index, highs):
    ncoord, slots = grad.shape
    return pl.pallas_call(
        _scatter_kernel,
        out_shape=jax.ShapeDtypeStruct((ncoord * LANES, highs), jnp.float32),
        scratch_shapes=[pltpu.VMEM((3 * ncoord * LANES, highs), jnp.float32)],
    )(grad, index.reshape(1, slots))


@functools.partial(jax.custom_vjp, nondiff_argnums=(2,))
def take_points(table, index, highs):
    return gather_points(table, index)


def _take_fwd(table, index, highs):
    return gather_points(table, index), index


def _take_bwd(highs, index, grad):
    return scatter_points(grad, index, highs), None


take_points.defvjp(_take_fwd, _take_bwd)


def project(camera_tile, point_obs, observed):
    axis_angle = camera_tile[0:3]
    theta_sq = jnp.sum(axis_angle * axis_angle, axis=0)
    sine_term = (
        1.0
        - theta_sq / 6.0
        + theta_sq * theta_sq / 120.0
        - theta_sq * theta_sq * theta_sq / 5040.0
        + theta_sq * theta_sq * theta_sq * theta_sq / 362880.0
    )
    cosine_term = (
        0.5
        - theta_sq / 24.0
        + theta_sq * theta_sq / 720.0
        - theta_sq * theta_sq * theta_sq / 40320.0
        + theta_sq * theta_sq * theta_sq * theta_sq / 3628800.0
    )
    crossed = jnp.stack(
        [
            axis_angle[1] * point_obs[2] - axis_angle[2] * point_obs[1],
            axis_angle[2] * point_obs[0] - axis_angle[0] * point_obs[2],
            axis_angle[0] * point_obs[1] - axis_angle[1] * point_obs[0],
        ]
    )
    inner = jnp.sum(axis_angle * point_obs, axis=0)
    camera_frame = (
        point_obs
        + sine_term * crossed
        + cosine_term * (axis_angle * inner - theta_sq * point_obs)
        + camera_tile[3:6]
    )
    horizontal = camera_frame[0] / camera_frame[2]
    vertical = camera_frame[1] / camera_frame[2]
    radius_sq = horizontal * horizontal + vertical * vertical
    scale_term = camera_tile[6] * (
        1.0 + camera_tile[7] * radius_sq + camera_tile[8] * radius_sq * radius_sq
    )
    return jnp.stack([scale_term * horizontal - observed[0], scale_term * vertical - observed[1]])


def reweight(residual):
    return 1.0 / (1.0 + residual[0] * residual[0] + residual[1] * residual[1])


def adam_step(current, moment_one, moment_two, gradient):
    moment_one = 0.9 * moment_one + 0.1 * gradient
    moment_two = 0.999 * moment_two + 0.001 * gradient * gradient
    corrected_one = moment_one / (1.0 - 0.9**STEP)
    corrected_two = moment_two / (1.0 - 0.999**STEP)
    return (
        current - 0.05 * corrected_one / (jnp.sqrt(corrected_two) + 1e-08),
        moment_one,
        moment_two,
    )


def on_device(
    cameras,
    cam_first,
    cam_second,
    points,
    pt_first,
    pt_second,
    observed,
    tile_camera,
    point_index,
    tile_count,
):
    tile_num = tile_count.shape[0]
    tile_len = observed.shape[1] // tile_num
    obs_grid = observed.reshape(2, tile_num, tile_len)
    slot = lax.broadcasted_iota(jnp.int32, (tile_num, tile_len), 1)
    valid_mask = (slot < tile_count[:, None]).astype(jnp.float32)

    def residuals(camera_block, point_block):
        camera_tile = jnp.take(camera_block, tile_camera, axis=1)[:, :, None]
        point_obs = take_points(point_block, point_index, point_block.shape[1]).reshape(3, tile_num, tile_len)
        return project(camera_tile, point_obs, obs_grid)

    cam_rows, cam_cols = cameras.shape
    pt_rows, pt_cols = points.shape
    n_pt = lax.axis_size("pt")
    n_cam = lax.axis_size("cam")

    def doubling_gather(local, axis_name, size):
        me = lax.axis_index(axis_name)
        buf = local[None]
        dist = 1
        while dist < size:
            pairs = [(i, i ^ dist) for i in range(size)]
            other = lax.ppermute(buf, axis_name, pairs)
            low_half = (me // dist) % 2 == 0
            buf = jnp.where(
                low_half,
                jnp.concatenate([buf, other], axis=0),
                jnp.concatenate([other, buf], axis=0),
            )
            dist *= 2
        return buf

    def butterfly_sum(value, axis_name, size):
        dist = 1
        while dist < size:
            pairs = [(i, i ^ dist) for i in range(size)]
            value = value + lax.ppermute(value, axis_name, pairs)
            dist *= 2
        return value

    def gather_pts(local):
        rows = local.shape[0]
        flat = local.reshape(rows * pt_cols // LANES, LANES)
        stacked = doubling_gather(flat, "cam", n_cam)
        stacked = stacked.reshape(n_cam, rows, pt_cols // LANES, LANES)
        return stacked.transpose(1, 3, 0, 2).reshape(rows * LANES, n_cam * pt_cols // LANES)

    def own_pts(table):
        parts = table.reshape(pt_rows, LANES, n_cam, pt_cols // LANES)
        mine = lax.dynamic_index_in_dim(parts, lax.axis_index("cam"), axis=2, keepdims=False)
        return mine.transpose(0, 2, 1).reshape(pt_rows, pt_cols)

    def own_cams(block):
        start = lax.axis_index("pt") * cam_cols
        return lax.dynamic_slice_in_dim(block, start, cam_cols, axis=1)

    cam_state = jnp.concatenate([cameras, cam_first, cam_second], axis=0)
    cam_state = doubling_gather(cam_state, "pt", n_pt)
    cam_state = cam_state.transpose(1, 0, 2).reshape(3, cam_rows, n_pt * cam_cols)
    camera_block, first_block, second_block = cam_state[0], cam_state[1], cam_state[2]
    point_block = gather_pts(points)
    residual, pullback = jax.vjp(residuals, camera_block, point_block)
    cotangent = residual * (reweight(residual) * valid_mask)
    camera_grad, point_grad = pullback(cotangent)
    camera_grad = butterfly_sum(
        camera_grad.reshape(cam_rows * n_pt, cam_cols), "pt", n_pt
    ).reshape(cam_rows, n_pt * cam_cols)
    point_grad = butterfly_sum(point_grad, "cam", n_cam)
    new_cam_block, new_cam_first, new_cam_second = adam_step(
        camera_block, first_block, second_block, camera_grad
    )
    moments = gather_pts(jnp.concatenate([pt_first, pt_second], axis=0))
    moments = moments.reshape(2, pt_rows * LANES, moments.shape[1])
    new_pt_block, new_pt_first, new_pt_second = adam_step(
        point_block, moments[0], moments[1], point_grad
    )
    new_cameras = own_cams(new_cam_block)
    new_cam_first = own_cams(new_cam_first)
    new_cam_second = own_cams(new_cam_second)
    new_points = own_pts(new_pt_block)
    new_pt_first = own_pts(new_pt_first)
    new_pt_second = own_pts(new_pt_second)
    final = residuals(new_cam_block, new_pt_block)
    final_weight = (reweight(final) * valid_mask).reshape(-1)
    final_residual = (final * valid_mask).reshape(2, -1)
    return (
        new_cameras,
        new_cam_first,
        new_cam_second,
        new_points,
        new_pt_first,
        new_pt_second,
        final_residual,
        final_weight,
    )


def solution(mesh):
    placed = (
        P(None, ("cam", "pt")),
        P(None, ("cam", "pt")),
        P(None, ("cam", "pt")),
        P(None, ("pt", "cam")),
        P(None, ("pt", "cam")),
        P(None, ("pt", "cam")),
        P(None, ("cam", "pt")),
        P(("cam", "pt")),
        P(("cam", "pt")),
        P(("cam", "pt")),
    )
    return jax.shard_map(
        on_device,
        mesh=mesh,
        in_specs=placed,
        out_specs=(
            P(None, ("cam", "pt")),
            P(None, ("cam", "pt")),
            P(None, ("cam", "pt")),
            P(None, ("pt", "cam")),
            P(None, ("pt", "cam")),
            P(None, ("pt", "cam")),
            P(None, ("cam", "pt")),
            P(("cam", "pt")),
        ),
        check_vma=False,
    )
```
